128 devices in a mesh: dp: 32 (over z, x, core), blk: 4 (over y).
Axes of the slice: x: 4, y: 4, z: 4, core: 2. Of those that a mesh axis runs over, the one named last changes fastest.
Arguments:
- embeddings: bfloat16 [32768, 768], P(('dp', 'blk')), may hold values from -6 to 6
- point_group: int32 [32768, 1], P(('dp', 'blk')), may hold values from 0 to 31; in each aligned block of 256 rows (0 to 255, 256 to 511, ...) at most 16 rows name the same one
- point_cluster: int32 [32768], P(('dp', 'blk')), may hold values from 0 to 31
- point_order: int32 [32768], P(('dp', 'blk')), may hold values from 0 to 32767, each once
Outputs:
- nearest: float32 [32768], P(('dp', 'blk'))
The draws below stay inside these ranges and needn't reach their ends.
Inputs may be any that keep to these rules, and one draw needn't show every extreme that they name: `point_group`: among the rows of one device at most 16 name the same group, a bound that some blocks reach. `point_order`: every value appears once.
All inputs are finite; a program needn't handle non-finite values.
Results may differ from the reference program's by a relative error of at most 0.00077.
Values may be sent and summed in bfloat16 or wider, within the bound.
No kernel may reach another device: no remote copies, remote signals or barrier semaphores. Data moves between devices by JAX's collectives and lax.ppermute only.
A program may use at most 64 MiB of HBM per device.

```python
import math
import jax
import jax.numpy as jnp
import numpy as np
from jax import lax

D = 768
PTS_DEV = 256
CLG = 32
POINTS = 32768
CAP = 16
GROUP_ROWS = 2048
N_DP = 32


def touch_ends(array, own_key, least, high):
    spot = [jax.random.randint(jax.random.fold_in(own_key, axis), (), 0, length) for axis, length in enumerate(array.shape)]
    main_axis = array.shape.index(max(array.shape))
    next_to = spot[:main_axis] + [(spot[main_axis] + 1) % array.shape[main_axis]] + spot[main_axis + 1:]
    return array.at[tuple(spot)].set(least).at[tuple(next_to)].set(high)


def levels(rng, dims, pieces, smallest, top_value):
    gain = 1.0
    for axis_at, shards_of in pieces:
        steps = jax.random.uniform(jax.random.fold_in(jax.random.fold_in(rng, 6), axis_at), (shards_of,), jnp.float32, smallest / len(pieces), top_value / len(pieces))
        gain = gain * jnp.repeat(jnp.exp(steps), dims[axis_at] // shards_of).reshape((-1,) + (1,) * (len(dims) - 1 - axis_at))
    return gain


def assign_block(rng, own, number, rows, count, top, bound, slope):
    ranking = jax.random.permutation(rng, count)
    crowded, common = portions_of(count, rows * top, bound, slope, True), portions_of(count, rows * top, bound, slope, False)
    places = jnp.arange(count)

    def named(sizes, offset_by):
        used = int((sizes > 0).sum())
        fixed = max(1, used // 4)
        moved = fixed + (places - fixed + offset_by * (used - fixed)) % max(1, count - fixed)
        return jnp.zeros((count,), jnp.int32).at[ranking[jnp.where(places < fixed, places, moved)]].set(jnp.asarray(sizes, jnp.int32))

    sizes = jnp.where(number % 4 == 0, named(crowded, number // 4), named(common, number - number // 4 - 1))
    mixed = jax.random.permutation(jax.random.fold_in(own, 3), count)
    donor, receiver = mixed[0:count // 2 * 2:2], mixed[1:count // 2 * 2:2]
    slack = jnp.minimum(sizes[donor] - 1, bound - sizes[receiver]) // 2
    slack = jnp.where((donor == ranking[0]) | (receiver == ranking[0]) | (sizes[receiver] == 0), 0, jnp.maximum(slack, 0))
    moved = jax.random.randint(jax.random.fold_in(own, 4), (count // 2,), 0, 1 << 20) % (slack + 1)
    sizes = sizes.at[donor].add(-moved).at[receiver].add(moved)
    items = jnp.searchsorted(jnp.cumsum(sizes), jnp.arange(rows * top), side="right").astype(jnp.int32)
    grid = items.reshape(top, rows).T
    grid = grid[jax.random.permutation(jax.random.fold_in(own, 1), rows)]
    offset_by = jax.random.randint(jax.random.fold_in(own, 2), (rows, 1), 0, top)
    return jnp.take_along_axis(grid, (jnp.arange(top)[None, :] + offset_by) % top, axis=1)


def portions_of(number_of, total, reach, skew, full):
    loads = [(1 << 20) // math.isqrt(rank ** skew) + 1 for rank in range(1, number_of + 1)]
    largest = reach if full else min(reach, max(-(-total // number_of), total * loads[0] // sum(loads)))
    least = 1 if total - largest >= number_of - 1 else 0
    given, spare = [largest] + [least] * (number_of - 1), total - largest - least * (number_of - 1)
    while spare > 0:
        candidates = [i for i in range(1, number_of) if given[i] < largest] or [i for i in range(1, number_of) if given[i] < reach]
        mass, budget = sum([loads[i] for i in candidates]), spare
        for i in candidates:
            extra = min(reach - given[i], max(1, budget * loads[i] // mass), spare)
            given[i] = given[i] + extra
            spare = spare - extra
    return np.array(given)


def scatter_about(own_key, shape, scale, reach, split=(), held_as=jnp.bfloat16):
    drawn = jax.random.normal(own_key, shape, jnp.float32) * scale
    if len(split) > 0:
        drawn = levels(own_key, shape, split, -0.22, 0.18) * drawn
    return jnp.clip(drawn, min=-reach, max=reach).astype(held_as)


def setup_inputs(seed: int = 0) -> dict:
    key_of = jax.random.split(jax.random.key(seed), 5)
    embeddings = scatter_about(key_of[0], (POINTS, D), 1.0, 6.0, ((0, 128),))
    point_group_keys = jax.random.split(jax.random.fold_in(key_of[1], 1), POINTS // PTS_DEV)
    point_group_turns = jax.random.permutation(jax.random.fold_in(key_of[1], 3), POINTS // PTS_DEV)
    point_group = jax.vmap(lambda own, number: assign_block(jax.random.fold_in(key_of[1], 2), own, number, PTS_DEV, N_DP, 1, CAP, 1))(point_group_keys, point_group_turns).reshape((POINTS, 1))
    point_cluster = touch_ends(jax.random.randint(key_of[2], (POINTS,), 0, CLG), jax.random.fold_in(key_of[2], 1), 0, CLG - 1).astype(jnp.int32)
    point_order = jax.random.permutation(key_of[3], POINTS).astype(jnp.int32)
    return dict(embeddings=embeddings, point_group=point_group, point_cluster=point_cluster, point_order=point_order)


def reference(embeddings, point_group, point_cluster, point_order):
    values = embeddings.astype(jnp.float32)
    scale = lax.rsqrt(lax.optimization_barrier(jnp.mean(values * values, axis=1, keepdims=True)) + 1e-06)
    unit = (values * scale * D ** (-0.5)).astype(jnp.bfloat16)
    group = point_group[:, 0].astype(jnp.int32)
    labels = group * CLG + point_cluster.astype(jnp.int32)
    order = point_order.astype(jnp.int32)
    perm = jnp.argsort(group, stable=True).astype(jnp.int32)
    member = (group[:, None] == jnp.arange(N_DP, dtype=jnp.int32)[None, :]).astype(jnp.int32)
    counts = lax.optimization_barrier(jnp.sum(member, axis=0)).astype(jnp.int32)
    starts = (jnp.cumsum(counts) - counts).astype(jnp.int32)
    pad_unit = jnp.concatenate([unit[perm], jnp.zeros((GROUP_ROWS, D), jnp.bfloat16)], axis=0)
    pad_labels = jnp.concatenate([labels[perm], jnp.full((GROUP_ROWS,), -1, jnp.int32)], axis=0)
    pad_order = jnp.concatenate([order[perm], jnp.zeros((GROUP_ROWS,), jnp.int32)], axis=0)

    def one_group(index):
        first = starts[index].astype(jnp.int32)
        rows = lax.dynamic_slice_in_dim(pad_unit, first, GROUP_ROWS, 0).astype(jnp.float32)
        group_labels = lax.dynamic_slice_in_dim(pad_labels, first, GROUP_ROWS, 0)
        group_order = lax.dynamic_slice_in_dim(pad_order, first, GROUP_ROWS, 0)
        valid = jnp.arange(GROUP_ROWS, dtype=jnp.int32) < counts[index]
        group_labels = jnp.where(valid, group_labels, -1)
        scores = jnp.dot(rows, rows.T, precision=lax.Precision.HIGHEST, preferred_element_type=jnp.float32)
        mask = (group_labels[:, None] == group_labels[None, :]) & (group_order[None, :] < group_order[:, None]) & valid[:, None]
        best = lax.optimization_barrier(jnp.max(jnp.where(mask, scores, -2.0), axis=1))
        return jnp.where(best > -1.5, best, -1.0)
    table = lax.map(one_group, jnp.arange(N_DP, dtype=jnp.int32))
    sorted_group = group[perm]
    position = jnp.arange(POINTS, dtype=jnp.int32) - starts[sorted_group]
    sorted_best = table[sorted_group, position]
    return jnp.zeros((POINTS,), jnp.float32).at[perm].set(sorted_best)
```

```python
import numpy as np
import jax
import jax.numpy as jnp
from jax import lax
from jax.sharding import PartitionSpec as P

CLG = 32
EXTRA = 128


def normalize(embeddings):
    values = embeddings.astype(jnp.float32)
    scale = lax.rsqrt(jnp.mean(values * values, axis=1, keepdims=True) + 1e-06)
    width = embeddings.shape[1]
    return (values * scale * width ** (-0.5)).astype(jnp.bfloat16)


def layout(zs, xs, ys):
    def lin(z, x, c, y):
        return ((z * xs + x) * 2 + c) * ys + y

    count = zs * xs * 2 * ys
    dev_of = np.zeros((zs * xs + zs * ys, 4), np.int32)
    nxt = np.zeros(count, np.int32)
    for z in range(zs):
        for x in range(xs):
            for y in range(ys):
                dev_of[z * xs + x, y] = lin(z, x, 0, y)
                dev_of[zs * xs + z * ys + y, x] = lin(z, x, 1, y)
                nxt[lin(z, x, 0, y)] = lin(z, x, 0, (y + 1) % ys)
                nxt[lin(z, x, 1, y)] = lin(z, (x + 1) % xs, 1, y)
    return dev_of, nxt


def strongest(query, keys):
    query_rows, query_cluster, query_order = query
    key_rows, key_cluster, key_order = keys
    count = key_rows.shape[0]
    step = 512
    tiles = (
        key_rows.reshape(count // step, step, key_rows.shape[1]),
        key_cluster.reshape(count // step, step),
        key_order.reshape(count // step, step),
    )

    def visit(best, block):
        rows, cluster, order = block
        scores = lax.dot_general(
            query_rows, rows, (((1,), (1,)), ((), ())), preferred_element_type=jnp.float32
        )
        mask = (query_cluster[:, None] == cluster[None, :]) & (order[None, :] < query_order[:, None])
        return (jnp.maximum(best, jnp.max(jnp.where(mask, scores, -2.0), axis=1)), None)

    init = jnp.full((query_rows.shape[0],), -2.0, jnp.float32)
    best, unused = lax.scan(visit, init, tiles)
    return best


def split_meta(rows, width):
    cluster = rows[:, width].astype(jnp.float32)
    order = rows[:, width + 1].astype(jnp.float32) * 256.0 + rows[:, width + 2].astype(jnp.float32)
    return rows[:, :width], cluster, order


def body(embeddings, point_group, point_cluster, point_order, dev_of, nxt):
    devices = nxt.shape[0]
    width = embeddings.shape[1]
    unit = normalize(embeddings)
    group = point_group[:, 0]
    groups = dev_of.shape[0]
    onehot = (group[:, None] == jnp.arange(groups, dtype=jnp.int32)[None, :]).astype(jnp.int32)
    before = jnp.cumsum(onehot, axis=0) - onehot
    rank = jnp.sum(before * onehot, axis=1)
    target = jnp.asarray(dev_of)[group, rank // 4] * 4 + rank % 4
    meta = jnp.stack(
        [point_cluster, point_order // 256, point_order % 256], axis=1
    ).astype(jnp.bfloat16)
    packed = jnp.concatenate(
        [unit, meta, jnp.zeros((unit.shape[0], EXTRA - 3), jnp.bfloat16)], axis=1
    )
    empty = jnp.zeros((devices * 4, width + EXTRA), jnp.bfloat16).at[:, width].set(-1.0)
    send = empty.at[target].set(packed)
    own = lax.all_to_all(send, ("dp", "blk"), split_axis=0, concat_axis=0, tiled=True)
    forward = [(i, int(nxt[i])) for i in range(devices)]
    backward = [(int(nxt[i]), i) for i in range(devices)]
    from_prev = lax.ppermute(own, ("dp", "blk"), forward)
    from_next = lax.ppermute(own, ("dp", "blk"), backward)
    half = own.shape[0] // 2
    far_a = lax.ppermute(from_next[:half], ("dp", "blk"), backward)
    far_b = lax.ppermute(from_prev[half:], ("dp", "blk"), forward)
    keys = jnp.concatenate([own, from_prev, from_next, far_a, far_b], axis=0)
    best = strongest(split_meta(own, width), split_meta(keys, width))
    answer = jnp.where(best > -1.5, best, -1.0)
    returned = lax.all_to_all(answer, ("dp", "blk"), split_axis=0, concat_axis=0, tiled=True)
    return returned[target]


def solution(mesh):
    zs, xs, ys = 4, 4, 4
    dev_of, nxt = layout(zs, xs, ys)
    in_specs = (P(("dp", "blk"), None), P(("dp", "blk"), None), P(("dp", "blk")), P(("dp", "blk")))
    out_specs = P(("dp", "blk"))

    def run(embeddings, point_group, point_cluster, point_order):
        return body(embeddings, point_group, point_cluster, point_order, dev_of, nxt)

    return jax.shard_map(run, mesh=mesh, in_specs=in_specs, out_specs=out_specs, check_vma=False)
```

```python
import numpy as np
import jax
import jax.numpy as jnp
from jax import lax
from jax.sharding import PartitionSpec as P

EXTRA = 128


def normalize(embeddings):
    values = embeddings.astype(jnp.float32)
    scale = lax.rsqrt(jnp.mean(values * values, axis=1, keepdims=True) + 1e-06)
    width = embeddings.shape[1]
    return (values * scale * width ** (-0.5)).astype(jnp.bfloat16)


def ring_of(zs, xs, ys):
    def lin(z, x, c, y):
        return ((z * xs + x) * 2 + c) * ys + y

    nxt = np.zeros(zs * xs * 2 * ys, np.int32)
    for z in range(zs):
        for x in range(xs):
            for y in range(ys):
                nxt[lin(z, x, 0, y)] = lin(z, x, 0, (y + 1) % ys)
                nxt[lin(z, x, 1, y)] = lin(z, (x + 1) % xs, 1, y)
    return nxt


def device_of(group, place, zs, xs, ys):
    first = group * 2 * ys + place
    other = group - zs * xs
    second = ((other // ys * xs + place) * 2 + 1) * ys + other % ys
    return jnp.where(group < zs * xs, first, second)


def split_meta(rows, width):
    cluster = rows[:, width].astype(jnp.float32) - 1.0
    order = rows[:, width + 1].astype(jnp.float32) * 256.0 + rows[:, width + 2].astype(jnp.float32)
    return rows[:, :width], cluster, order


def best_over(query, keys):
    query_rows, query_cluster, query_order = query
    key_rows, key_cluster, key_order = keys
    scores = lax.dot_general(
        query_rows, key_rows, (((1,), (1,)), ((), ())), preferred_element_type=jnp.float32
    )
    mask = (query_cluster[:, None] == key_cluster[None, :]) & (key_order[None, :] < query_order[:, None])
    return jnp.max(jnp.where(mask, scores, -2.0), axis=1)


def body(embeddings, point_group, point_cluster, point_order, nxt, dims):
    zs, xs, ys = dims
    devices = nxt.shape[0]
    points, width = embeddings.shape
    slots = devices * 4
    unit = normalize(embeddings)
    group = point_group[:, 0]
    index = jnp.arange(points, dtype=jnp.int32)
    same = (group[:, None] == group[None, :]) & (index[None, :] < index[:, None])
    rank = jnp.sum(same.astype(jnp.int32), axis=1)
    target = device_of(group, rank // 4, zs, xs, ys) * 4 + rank % 4
    meta = jnp.stack(
        [point_cluster + 1, point_order // 256, point_order % 256], axis=1
    ).astype(jnp.bfloat16)
    packed = jnp.concatenate(
        [unit, meta, jnp.zeros((points, EXTRA - 3), jnp.bfloat16)], axis=1
    )
    place = (target[None, :] == jnp.arange(slots, dtype=jnp.int32)[:, None]).astype(jnp.bfloat16)
    send = lax.dot_general(
        place, packed, (((1,), (0,)), ((), ())), preferred_element_type=jnp.float32
    ).astype(jnp.bfloat16)
    own = lax.all_to_all(send, ("dp", "blk"), split_axis=0, concat_axis=0, tiled=True)
    forward = [(i, int(nxt[i])) for i in range(devices)]
    backward = [(int(nxt[i]), i) for i in range(devices)]
    from_prev = lax.ppermute(own, ("dp", "blk"), forward)
    from_next = lax.ppermute(own, ("dp", "blk"), backward)
    half = own.shape[0] // 2
    far_a = lax.ppermute(from_next[:half], ("dp", "blk"), backward)
    far_b = lax.ppermute(from_prev[half:], ("dp", "blk"), forward)
    query = split_meta(own, width)
    best = best_over(query, query)
    best = jnp.maximum(best, best_over(query, split_meta(from_prev, width)))
    best = jnp.maximum(best, best_over(query, split_meta(from_next, width)))
    best = jnp.maximum(best, best_over(query, split_meta(far_a, width)))
    best = jnp.maximum(best, best_over(query, split_meta(far_b, width)))
    answer = jnp.where(best > -1.5, best, -1.0)
    returned = lax.all_to_all(answer, ("dp", "blk"), split_axis=0, concat_axis=0, tiled=True)
    pick = target[:, None] == jnp.arange(slots, dtype=jnp.int32)[None, :]
    return jnp.max(jnp.where(pick, returned[None, :], -jnp.inf), axis=1)


def solution(mesh):
    dims = (4, 4, 4)
    nxt = ring_of(*dims)
    in_specs = (P(("dp", "blk"), None), P(("dp", "blk"), None), P(("dp", "blk")), P(("dp", "blk")))
    out_specs = P(("dp", "blk"))

    def run(embeddings, point_group, point_cluster, point_order):
        return body(embeddings, point_group, point_cluster, point_order, nxt, dims)

    return jax.shard_map(run, mesh=mesh, in_specs=in_specs, out_specs=out_specs, check_vma=False)
```

```python
import numpy as np
import jax
import jax.numpy as jnp
from jax import lax
from jax.sharding import PartitionSpec as P

EXTRA = 128


def normalize(embeddings):
    values = embeddings.astype(jnp.float32)
    scale = lax.rsqrt(jnp.mean(values * values, axis=1, keepdims=True) + 1e-06)
    width = embeddings.shape[1]
    return (values * scale * width ** (-0.5)).astype(jnp.bfloat16)


def ring_of(zs, xs, ys):
    def lin(z, x, c, y):
        return ((z * xs + x) * 2 + c) * ys + y

    nxt = np.zeros(zs * xs * 2 * ys, np.int32)
    for z in range(zs):
        for x in range(xs):
            for y in range(ys):
                nxt[lin(z, x, 0, y)] = lin(z, x, 0, (y + 1) % ys)
                nxt[lin(z, x, 1, y)] = lin(z, (x + 1) % xs, 1, y)
    return nxt


def device_of(group, place, zs, xs, ys):
    first = group * 2 * ys + place
    other = group - zs * xs
    second = ((other // ys * xs + place) * 2 + 1) * ys + other % ys
    return jnp.where(group < zs * xs, first, second)


def split_meta(rows, width):
    cluster = rows[:, width].astype(jnp.float32) - 1.0
    order = rows[:, width + 1].astype(jnp.float32) * 256.0 + rows[:, width + 2].astype(jnp.float32)
    return rows[:, :width], cluster, order


def best_over(query, keys):
    query_rows, query_cluster, query_order = query
    key_rows, key_cluster, key_order = keys
    scores = lax.dot_general(
        query_rows, key_rows, (((1,), (1,)), ((), ())), preferred_element_type=jnp.float32
    )
    mask = (query_cluster[:, None] == key_cluster[None, :]) & (key_order[None, :] < query_order[:, None])
    return jnp.max(jnp.where(mask, scores, -2.0), axis=1)


def body(embeddings, point_group, point_cluster, point_order, nxt, dims):
    zs, xs, ys = dims
    devices = nxt.shape[0]
    points, width = embeddings.shape
    slots = devices * 4
    unit = normalize(embeddings)
    group = point_group[:, 0]
    index = jnp.arange(points, dtype=jnp.int32)
    same = (group[:, None] == group[None, :]) & (index[None, :] < index[:, None])
    rank = jnp.sum(same.astype(jnp.int32), axis=1)
    target = device_of(group, rank // 4, zs, xs, ys) * 4 + rank % 4
    meta = jnp.stack(
        [point_cluster + 1, point_order // 256, point_order % 256], axis=1
    ).astype(jnp.bfloat16)
    packed = jnp.concatenate(
        [unit, meta, jnp.zeros((points, EXTRA - 3), jnp.bfloat16)], axis=1
    )
    place = (target[None, :] == jnp.arange(slots, dtype=jnp.int32)[:, None]).astype(jnp.bfloat16)
    send = lax.dot_general(
        place, packed, (((1,), (0,)), ((), ())), preferred_element_type=jnp.float32
    ).astype(jnp.bfloat16)
    own = lax.all_to_all(send, ("dp", "blk"), split_axis=0, concat_axis=0, tiled=True)
    forward = [(i, int(nxt[i])) for i in range(devices)]
    backward = [(int(nxt[i]), i) for i in range(devices)]
    half = own.shape[0] // 2
    own_a, own_b = own[:half], own[half:]
    prev_b = lax.ppermute(own_b, ("dp", "blk"), forward)
    next_a = lax.ppermute(own_a, ("dp", "blk"), backward)
    prev_a = lax.ppermute(own_a, ("dp", "blk"), forward)
    next_b = lax.ppermute(own_b, ("dp", "blk"), backward)
    far_b = lax.ppermute(prev_b, ("dp", "blk"), forward)
    far_a = lax.ppermute(next_a, ("dp", "blk"), backward)
    query = split_meta(own, width)
    best = best_over(query, query)
    for block in (prev_b, next_a, prev_a, next_b, far_b, far_a):
        best = jnp.maximum(best, best_over(query, split_meta(block, width)))
    answer = jnp.where(best > -1.5, best, -1.0)
    returned = lax.all_to_all(
        answer.reshape(devices, 4), ("dp", "blk"), split_axis=0, concat_axis=0, tiled=False
    ).reshape(slots)
    pick = target[:, None] == jnp.arange(slots, dtype=jnp.int32)[None, :]
    return jnp.max(jnp.where(pick, returned[None, :], -jnp.inf), axis=1)


def solution(mesh):
    dims = (4, 4, 4)
    nxt = ring_of(*dims)
    in_specs = (P(("dp", "blk"), None), P(("dp", "blk"), None), P(("dp", "blk")), P(("dp", "blk")))
    out_specs = P(("dp", "blk"))

    def run(embeddings, point_group, point_cluster, point_order):
        return body(embeddings, point_group, point_cluster, point_order, nxt, dims)

    return jax.shard_map(run, mesh=mesh, in_specs=in_specs, out_specs=out_specs, check_vma=False)
```

```python
import numpy as np
import jax
import jax.numpy as jnp
from jax import lax
from jax.sharding import PartitionSpec as P

EXTRA = 128


def normalize(embeddings):
    values = embeddings.astype(jnp.float32)
    scale = lax.rsqrt(jnp.mean(values * values, axis=1, keepdims=True) + 1e-06)
    width = embeddings.shape[1]
    return (values * scale * width ** (-0.5)).astype(jnp.bfloat16)


def ring_of(zs, xs, ys):
    def lin(z, x, c, y):
        return ((z * xs + x) * 2 + c) * ys + y

    nxt = np.zeros(zs * xs * 2 * ys, np.int32)
    ring_pos = np.zeros(zs * xs * 2 * ys, np.int32)
    for z in range(zs):
        for x in range(xs):
            for y in range(ys):
                nxt[lin(z, x, 0, y)] = lin(z, x, 0, (y + 1) % ys)
                nxt[lin(z, x, 1, y)] = lin(z, (x + 1) % xs, 1, y)
                ring_pos[lin(z, x, 0, y)] = y
                ring_pos[lin(z, x, 1, y)] = x
    return nxt, ring_pos


def device_of(group, place, zs, xs, ys):
    first = group * 2 * ys + place
    other = group - zs * xs
    second = ((other // ys * xs + place) * 2 + 1) * ys + other % ys
    return jnp.where(group < zs * xs, first, second)


def split_meta(rows, width):
    cluster = rows[:, width].astype(jnp.float32) - 1.0
    order = rows[:, width + 1].astype(jnp.float32) * 256.0 + rows[:, width + 2].astype(jnp.float32)
    return rows[:, :width], cluster, order


def masks(query, keys):
    query_rows, query_cluster, query_order = query
    key_rows, key_cluster, key_order = keys
    scores = lax.dot_general(
        query_rows, key_rows, (((1,), (1,)), ((), ())), preferred_element_type=jnp.float32
    )
    same = query_cluster[:, None] == key_cluster[None, :]
    return scores, same, key_order[None, :] < query_order[:, None]


def best_over(query, keys):
    scores, same, earlier = masks(query, keys)
    return jnp.max(jnp.where(same & earlier, scores, -2.0), axis=1)


def body(embeddings, point_group, point_cluster, point_order, nxt, ring_pos, dims):
    zs, xs, ys = dims
    devices = nxt.shape[0]
    points, width = embeddings.shape
    slots = devices * 4
    unit = normalize(embeddings)
    group = point_group[:, 0]
    index = jnp.arange(points, dtype=jnp.int32)
    same = (group[:, None] == group[None, :]) & (index[None, :] < index[:, None])
    rank = jnp.sum(same.astype(jnp.int32), axis=1)
    place = rank // 4
    target = device_of(group, place, zs, xs, ys) * 4 + rank % 4
    meta = jnp.stack(
        [point_cluster + 1, point_order // 256, point_order % 256], axis=1
    ).astype(jnp.bfloat16)
    packed = jnp.concatenate(
        [unit, meta, jnp.zeros((points, EXTRA - 3), jnp.bfloat16)], axis=1
    )
    spot = (target[None, :] == jnp.arange(slots, dtype=jnp.int32)[:, None]).astype(jnp.bfloat16)
    send = lax.dot_general(
        spot, packed, (((1,), (0,)), ((), ())), preferred_element_type=jnp.float32
    ).astype(jnp.bfloat16)
    own = lax.all_to_all(send, ("dp", "blk"), split_axis=0, concat_axis=0, tiled=True)
    forward = [(i, int(nxt[i])) for i in range(devices)]
    backward = [(int(nxt[i]), i) for i in range(devices)]
    prev = lax.ppermute(own, ("dp", "blk"), forward)
    next_ = lax.ppermute(own, ("dp", "blk"), backward)
    query = split_meta(own, width)
    best = best_over(query, query)
    best = jnp.maximum(best, best_over(query, split_meta(prev, width)))
    best = jnp.maximum(best, best_over(query, split_meta(next_, width)))
    half = slots // 2
    me = jnp.asarray(ring_pos)[lax.axis_index(("dp", "blk"))]
    inner = (me == 1) | (me == 2)
    rows = jnp.where(inner, prev[:half], next_[half:])
    cols = jnp.where(inner, next_, prev)
    scores, same_c, earlier = masks(split_meta(rows, width), split_meta(cols, width))
    row_part = jnp.max(jnp.where(same_c & earlier, scores, -2.0), axis=1)
    col_order_r = split_meta(rows, width)[2]
    col_order_c = split_meta(cols, width)[2]
    col_ok = same_c & (col_order_r[:, None] < col_order_c[None, :])
    col_part = jnp.max(jnp.where(col_ok, scores, -2.0), axis=0)
    floor = jnp.full((half,), -2.0, jnp.float32)
    side_prev = jnp.where(inner, jnp.concatenate([row_part, floor]), col_part)
    side_next = jnp.where(inner, col_part, jnp.concatenate([floor, row_part]))
    payload = jnp.stack(
        [best.reshape(devices, 4), side_prev.reshape(devices, 4), side_next.reshape(devices, 4)],
        axis=1,
    ).reshape(devices, 12)
    returned = lax.all_to_all(
        payload, ("dp", "blk"), split_axis=0, concat_axis=0, tiled=True
    ).reshape(devices * 12)
    lane = rank % 4
    at_own = device_of(group, place, zs, xs, ys) * 12 + lane
    at_prev = device_of(group, (place + 3) % 4, zs, xs, ys) * 12 + 8 + lane
    at_next = device_of(group, (place + 1) % 4, zs, xs, ys) * 12 + 4 + lane
    entry = jnp.arange(devices * 12, dtype=jnp.int32)[None, :]
    pick = (entry == at_own[:, None]) | (entry == at_prev[:, None]) | (entry == at_next[:, None])
    found = jnp.max(jnp.where(pick, returned[None, :], -2.0), axis=1)
    return jnp.where(found > -1.5, found, -1.0)


def solution(mesh):
    dims = (4, 4, 4)
    nxt, ring_pos = ring_of(*dims)
    in_specs = (P(("dp", "blk"), None), P(("dp", "blk"), None), P(("dp", "blk")), P(("dp", "blk")))
    out_specs = P(("dp", "blk"))

    def run(embeddings, point_group, point_cluster, point_order):
        return body(embeddings, point_group, point_cluster, point_order, nxt, ring_pos, dims)

    return jax.shard_map(run, mesh=mesh, in_specs=in_specs, out_specs=out_specs, check_vma=False)
```

```python
import numpy as np
import jax
import jax.numpy as jnp
from jax import lax
from jax.sharding import PartitionSpec as P
from jax.experimental import pallas as pl

EXTRA = 128


def normalize(embeddings):
    values = embeddings.astype(jnp.float32)
    scale = lax.rsqrt(jnp.mean(values * values, axis=1, keepdims=True) + 1e-06)
    width = embeddings.shape[1]
    return (values * scale * width ** (-0.5)).astype(jnp.bfloat16)


def ring_of(zs, xs, ys):
    def lin(z, x, c, y):
        return ((z * xs + x) * 2 + c) * ys + y

    nxt = np.zeros(zs * xs * 2 * ys, np.int32)
    ring_pos = np.zeros(zs * xs * 2 * ys, np.int32)
    for z in range(zs):
        for x in range(xs):
            for y in range(ys):
                nxt[lin(z, x, 0, y)] = lin(z, x, 0, (y + 1) % ys)
                nxt[lin(z, x, 1, y)] = lin(z, (x + 1) % xs, 1, y)
                ring_pos[lin(z, x, 0, y)] = y
                ring_pos[lin(z, x, 1, y)] = x
    return nxt, ring_pos


def device_of(group, place, zs, xs, ys):
    first = group * 2 * ys + place
    other = group - zs * xs
    second = ((other // ys * xs + place) * 2 + 1) * ys + other % ys
    return jnp.where(group < zs * xs, first, second)


def place_of(group, place, zs, xs, ys):
    first = group * 2 * ys + place
    other = group - zs * xs
    second = (((other >> 2) * xs + place) * 2 + 1) * ys + (other & 3)
    return jnp.where(group < zs * xs, first, second)


def prologue(dims):
    zs, xs, ys = dims

    def kernel(emb_ref, meta_ref, send_ref, idx_ref):
        x = emb_ref[...].astype(jnp.float32)
        width = x.shape[1]
        points = x.shape[0]
        slots = send_ref.shape[0]
        scale = lax.rsqrt(jnp.mean(x * x, axis=1, keepdims=True) + 1e-06)
        unit = (x * scale * width ** (-0.5)).astype(jnp.bfloat16)
        rows = meta_ref[...]
        cols = rows.T
        group_col = cols[:, 3:4]
        below = lax.broadcasted_iota(jnp.int32, (points, points), 1) < lax.broadcasted_iota(
            jnp.int32, (points, points), 0
        )
        same = (group_col == rows[3:4, :]) & below
        rank = jnp.sum(same.astype(jnp.float32), axis=1, keepdims=True).astype(jnp.int32)
        group = group_col.astype(jnp.int32)
        place = rank >> 2
        lane = rank & 3
        dev = place_of(group, place, zs, xs, ys)
        target = dev * 4 + lane
        spot = (target == lax.broadcasted_iota(jnp.int32, (points, slots), 1)).astype(jnp.float32)
        spot = spot.T.astype(jnp.bfloat16)
        send_ref[:, :width] = jnp.dot(spot, unit, preferred_element_type=jnp.float32).astype(
            jnp.bfloat16
        )
        send_ref[:, width:] = jnp.dot(
            spot, cols.astype(jnp.bfloat16), preferred_element_type=jnp.float32
        ).astype(jnp.bfloat16)
        at_own = dev * 12 + lane
        at_prev = place_of(group, (place + 3) & 3, zs, xs, ys) * 12 + 8 + lane
        at_next = place_of(group, (place + 1) & 3, zs, xs, ys) * 12 + 4 + lane
        which = lax.broadcasted_iota(jnp.int32, idx_ref.shape, 1)
        idx_ref[...] = jnp.where(which == 0, at_own, jnp.where(which == 1, at_prev, at_next))

    return kernel


def build_send(embeddings, group, point_cluster, point_order, slots, dims, interpret=False):
    points, width = embeddings.shape
    meta = jnp.concatenate(
        [
            jnp.stack([point_cluster + 1, point_order // 256, point_order % 256, group]).astype(
                jnp.float32
            ),
            jnp.zeros((EXTRA - 4, points), jnp.float32),
        ]
    )
    return pl.pallas_call(
        prologue(dims),
        out_shape=(
            jax.ShapeDtypeStruct((slots, width + EXTRA), jnp.bfloat16),
            jax.ShapeDtypeStruct((points, 128), jnp.int32),
        ),
        interpret=interpret,
    )(embeddings, meta)


def split_meta(rows, width):
    cluster = rows[:, width].astype(jnp.float32) - 1.0
    order = rows[:, width + 1].astype(jnp.float32) * 256.0 + rows[:, width + 2].astype(jnp.float32)
    return rows[:, :width], cluster, order


def masks(query, keys):
    query_rows, query_cluster, query_order = query
    key_rows, key_cluster, key_order = keys
    scores = lax.dot_general(
        query_rows, key_rows, (((1,), (1,)), ((), ())), preferred_element_type=jnp.float32
    )
    same = query_cluster[:, None] == key_cluster[None, :]
    return scores, same, key_order[None, :] < query_order[:, None]


def best_over(query, keys):
    scores, same, earlier = masks(query, keys)
    return jnp.max(jnp.where(same & earlier, scores, -2.0), axis=1)


def body(embeddings, point_group, point_cluster, point_order, nxt, ring_pos, dims):
    zs, xs, ys = dims
    devices = nxt.shape[0]
    points, width = embeddings.shape
    slots = devices * 4
    group = point_group[:, 0]
    send, idx = build_send(embeddings, group, point_cluster, point_order, slots, dims)
    own = lax.all_to_all(send, ("dp", "blk"), split_axis=0, concat_axis=0, tiled=True)
    forward = [(i, int(nxt[i])) for i in range(devices)]
    backward = [(int(nxt[i]), i) for i in range(devices)]
    prev = lax.ppermute(own, ("dp", "blk"), forward)
    next_ = lax.ppermute(own, ("dp", "blk"), backward)
    query = split_meta(own, width)
    best = best_over(query, query)
    best = jnp.maximum(best, best_over(query, split_meta(prev, width)))
    best = jnp.maximum(best, best_over(query, split_meta(next_, width)))
    half = slots // 2
    me = jnp.asarray(ring_pos)[lax.axis_index(("dp", "blk"))]
    inner = (me == 1) | (me == 2)
    rows = jnp.where(inner, prev[:half], next_[half:])
    cols = jnp.where(inner, next_, prev)
    scores, same_c, earlier = masks(split_meta(rows, width), split_meta(cols, width))
    row_part = jnp.max(jnp.where(same_c & earlier, scores, -2.0), axis=1)
    col_order_r = split_meta(rows, width)[2]
    col_order_c = split_meta(cols, width)[2]
    col_ok = same_c & (col_order_r[:, None] < col_order_c[None, :])
    col_part = jnp.max(jnp.where(col_ok, scores, -2.0), axis=0)
    floor = jnp.full((half,), -2.0, jnp.float32)
    side_prev = jnp.where(inner, jnp.concatenate([row_part, floor]), col_part)
    side_next = jnp.where(inner, col_part, jnp.concatenate([floor, row_part]))
    payload = jnp.stack(
        [best.reshape(devices, 4), side_prev.reshape(devices, 4), side_next.reshape(devices, 4)],
        axis=1,
    ).reshape(devices, 12)
    returned = lax.all_to_all(
        payload, ("dp", "blk"), split_axis=0, concat_axis=0, tiled=True
    ).reshape(devices * 12)
    at_own, at_prev, at_next = idx[:, 0], idx[:, 1], idx[:, 2]
    entry = jnp.arange(devices * 12, dtype=jnp.int32)[None, :]
    pick = (entry == at_own[:, None]) | (entry == at_prev[:, None]) | (entry == at_next[:, None])
    found = jnp.max(jnp.where(pick, returned[None, :], -2.0), axis=1)
    return jnp.where(found > -1.5, found, -1.0)


def solution(mesh):
    dims = (4, 4, 4)
    nxt, ring_pos = ring_of(*dims)
    in_specs = (P(("dp", "blk"), None), P(("dp", "blk"), None), P(("dp", "blk")), P(("dp", "blk")))
    out_specs = P(("dp", "blk"))

    def run(embeddings, point_group, point_cluster, point_order):
        return body(embeddings, point_group, point_cluster, point_order, nxt, ring_pos, dims)

    return jax.shard_map(run, mesh=mesh, in_specs=in_specs, out_specs=out_specs, check_vma=False)
```

```python
import numpy as np
import jax
import jax.numpy as jnp
from jax import lax
from jax.sharding import PartitionSpec as P
from jax.experimental import pallas as pl

EXTRA = 128


def normalize(embeddings):
    values = embeddings.astype(jnp.float32)
    scale = lax.rsqrt(jnp.mean(values * values, axis=1, keepdims=True) + 1e-06)
    width = embeddings.shape[1]
    return (values * scale * width ** (-0.5)).astype(jnp.bfloat16)


def ring_of(zs, xs, ys):
    def lin(z, x, c, y):
        return ((z * xs + x) * 2 + c) * ys + y

    nxt = np.zeros(zs * xs * 2 * ys, np.int32)
    ring_pos = np.zeros(zs * xs * 2 * ys, np.int32)
    for z in range(zs):
        for x in range(xs):
            for y in range(ys):
                nxt[lin(z, x, 0, y)] = lin(z, x, 0, (y + 1) % ys)
                nxt[lin(z, x, 1, y)] = lin(z, (x + 1) % xs, 1, y)
                ring_pos[lin(z, x, 0, y)] = y
                ring_pos[lin(z, x, 1, y)] = x
    return nxt, ring_pos


def device_of(group, place, zs, xs, ys):
    first = group * 2 * ys + place
    other = group - zs * xs
    second = ((other // ys * xs + place) * 2 + 1) * ys + other % ys
    return jnp.where(group < zs * xs, first, second)


def place_of(group, place, zs, xs, ys):
    first = group * 2 * ys + place
    other = group - zs * xs
    second = (((other >> 2) * xs + place) * 2 + 1) * ys + (other & 3)
    return jnp.where(group < zs * xs, first, second)


def prologue(dims):
    zs, xs, ys = dims

    def kernel(emb_ref, group_ref, cluster_ref, order_ref, packed_ref, idx_ref):
        x = emb_ref[...].astype(jnp.float32)
        points, width = x.shape
        scale = lax.rsqrt(jnp.mean(x * x, axis=1, keepdims=True) + 1e-06)
        packed_ref[:, :width] = (x * scale * width ** (-0.5)).astype(jnp.bfloat16)
        group_row = group_ref[...]
        order_row = order_ref[...]
        shape = (packed_ref.shape[1] - width, points)
        which = lax.broadcasted_iota(jnp.int32, shape, 0)
        rows = jnp.where(
            which == 0,
            cluster_ref[...] + 1,
            jnp.where(
                which == 1,
                order_row >> 8,
                jnp.where(which == 2, order_row & 255, jnp.where(which == 3, group_row, 0)),
            ),
        ).astype(jnp.float32)
        cols = rows.T
        packed_ref[:, width:] = cols.astype(jnp.bfloat16)
        group_col = cols[:, 3:4]
        below = lax.broadcasted_iota(jnp.int32, (points, points), 1) < lax.broadcasted_iota(
            jnp.int32, (points, points), 0
        )
        same = (group_col == group_row.astype(jnp.float32)) & below
        rank = jnp.sum(same.astype(jnp.float32), axis=1, keepdims=True).astype(jnp.int32)
        group = group_col.astype(jnp.int32)
        place = rank >> 2
        lane = rank & 3
        dev = place_of(group, place, zs, xs, ys)
        at_prev = place_of(group, (place + 3) & 3, zs, xs, ys) * 12 + 8 + lane
        at_next = place_of(group, (place + 1) & 3, zs, xs, ys) * 12 + 4 + lane
        pick = lax.broadcasted_iota(jnp.int32, idx_ref.shape, 1)
        idx_ref[...] = jnp.where(
            pick == 0,
            dev * 4 + lane,
            jnp.where(pick == 1, dev * 12 + lane, jnp.where(pick == 2, at_prev, at_next)),
        )

    return kernel


def build_send(embeddings, group, point_cluster, point_order, slots, dims, interpret=False):
    points, width = embeddings.shape
    packed, idx = pl.pallas_call(
        prologue(dims),
        out_shape=(
            jax.ShapeDtypeStruct((points, width + EXTRA), jnp.bfloat16),
            jax.ShapeDtypeStruct((points, 128), jnp.int32),
        ),
        interpret=interpret,
    )(
        embeddings,
        group.reshape(1, points),
        point_cluster.reshape(1, points),
        point_order.reshape(1, points),
    )
    spot = (idx[:, 0][None, :] == jnp.arange(slots, dtype=jnp.int32)[:, None]).astype(jnp.bfloat16)
    send = lax.dot_general(
        spot, packed, (((1,), (0,)), ((), ())), preferred_element_type=jnp.float32
    ).astype(jnp.bfloat16)
    return send, idx[:, 1:4]


def split_meta(rows, width):
    cluster = rows[:, width].astype(jnp.float32) - 1.0
    order = rows[:, width + 1].astype(jnp.float32) * 256.0 + rows[:, width + 2].astype(jnp.float32)
    return rows[:, :width], cluster, order


def masks(query, keys):
    query_rows, query_cluster, query_order = query
    key_rows, key_cluster, key_order = keys
    scores = lax.dot_general(
        query_rows, key_rows, (((1,), (1,)), ((), ())), preferred_element_type=jnp.float32
    )
    same = query_cluster[:, None] == key_cluster[None, :]
    return scores, same, key_order[None, :] < query_order[:, None]


def best_over(query, keys):
    scores, same, earlier = masks(query, keys)
    return jnp.max(jnp.where(same & earlier, scores, -2.0), axis=1)


def body(embeddings, point_group, point_cluster, point_order, nxt, ring_pos, dims):
    zs, xs, ys = dims
    devices = nxt.shape[0]
    points, width = embeddings.shape
    slots = devices * 4
    group = point_group[:, 0]
    send, idx = build_send(embeddings, group, point_cluster, point_order, slots, dims)
    own = lax.all_to_all(send, ("dp", "blk"), split_axis=0, concat_axis=0, tiled=True)
    forward = [(i, int(nxt[i])) for i in range(devices)]
    backward = [(int(nxt[i]), i) for i in range(devices)]
    prev = lax.ppermute(own, ("dp", "blk"), forward)
    next_ = lax.ppermute(own, ("dp", "blk"), backward)
    query = split_meta(own, width)
    best = best_over(query, query)
    best = jnp.maximum(best, best_over(query, split_meta(prev, width)))
    best = jnp.maximum(best, best_over(query, split_meta(next_, width)))
    half = slots // 2
    me = jnp.asarray(ring_pos)[lax.axis_index(("dp", "blk"))]
    inner = (me == 1) | (me == 2)
    rows = jnp.where(inner, prev[:half], next_[half:])
    cols = jnp.where(inner, next_, prev)
    scores, same_c, earlier = masks(split_meta(rows, width), split_meta(cols, width))
    row_part = jnp.max(jnp.where(same_c & earlier, scores, -2.0), axis=1)
    col_order_r = split_meta(rows, width)[2]
    col_order_c = split_meta(cols, width)[2]
    col_ok = same_c & (col_order_r[:, None] < col_order_c[None, :])
    col_part = jnp.max(jnp.where(col_ok, scores, -2.0), axis=0)
    floor = jnp.full((half,), -2.0, jnp.float32)
    side_prev = jnp.where(inner, jnp.concatenate([row_part, floor]), col_part)
    side_next = jnp.where(inner, col_part, jnp.concatenate([floor, row_part]))
    payload = jnp.stack(
        [best.reshape(devices, 4), side_prev.reshape(devices, 4), side_next.reshape(devices, 4)],
        axis=1,
    ).reshape(devices, 12)
    returned = lax.all_to_all(
        payload, ("dp", "blk"), split_axis=0, concat_axis=0, tiled=True
    ).reshape(devices * 12)
    at_own, at_prev, at_next = idx[:, 0], idx[:, 1], idx[:, 2]
    entry = jnp.arange(devices * 12, dtype=jnp.int32)[None, :]
    pick = (entry == at_own[:, None]) | (entry == at_prev[:, None]) | (entry == at_next[:, None])
    found = jnp.max(jnp.where(pick, returned[None, :], -2.0), axis=1)
    return jnp.where(found > -1.5, found, -1.0)


def solution(mesh):
    dims = (4, 4, 4)
    nxt, ring_pos = ring_of(*dims)
    in_specs = (P(("dp", "blk"), None), P(("dp", "blk"), None), P(("dp", "blk")), P(("dp", "blk")))
    out_specs = P(("dp", "blk"))

    def run(embeddings, point_group, point_cluster, point_order):
        return body(embeddings, point_group, point_cluster, point_order, nxt, ring_pos, dims)

    return jax.shard_map(run, mesh=mesh, in_specs=in_specs, out_specs=out_specs, check_vma=False)
```

```python
import numpy as np
import jax
import jax.numpy as jnp
from jax import lax
from jax.sharding import PartitionSpec as P
from jax.experimental import pallas as pl

EXTRA = 128


def normalize(embeddings):
    values = embeddings.astype(jnp.float32)
    scale = lax.rsqrt(jnp.mean(values * values, axis=1, keepdims=True) + 1e-06)
    width = embeddings.shape[1]
    return (values * scale * width ** (-0.5)).astype(jnp.bfloat16)


def ring_of(zs, xs, ys):
    def lin(z, x, c, y):
        return ((z * xs + x) * 2 + c) * ys + y

    nxt = np.zeros(zs * xs * 2 * ys, np.int32)
    ring_pos = np.zeros(zs * xs * 2 * ys, np.int32)
    for z in range(zs):
        for x in range(xs):
            for y in range(ys):
                nxt[lin(z, x, 0, y)] = lin(z, x, 0, (y + 1) % ys)
                nxt[lin(z, x, 1, y)] = lin(z, (x + 1) % xs, 1, y)
                ring_pos[lin(z, x, 0, y)] = y
                ring_pos[lin(z, x, 1, y)] = x
    return nxt, ring_pos


def device_of(group, place, zs, xs, ys):
    first = group * 2 * ys + place
    other = group - zs * xs
    second = ((other // ys * xs + place) * 2 + 1) * ys + other % ys
    return jnp.where(group < zs * xs, first, second)


def place_of(group, place, zs, xs, ys):
    first = group * 2 * ys + place
    other = group - zs * xs
    second = (((other >> 2) * xs + place) * 2 + 1) * ys + (other & 3)
    return jnp.where(group < zs * xs, first, second)


def prologue(dims):
    zs, xs, ys = dims

    def kernel(emb_ref, group_ref, cluster_ref, order_ref, packed_ref, idx_ref):
        x = emb_ref[...].astype(jnp.float32)
        points, width = x.shape
        scale = lax.rsqrt(jnp.mean(x * x, axis=1, keepdims=True) + 1e-06)
        packed_ref[:, :width] = (x * scale * width ** (-0.5)).astype(jnp.bfloat16)
        group_row = group_ref[...]
        order_row = order_ref[...]
        shape = (packed_ref.shape[1] - width, points)
        which = lax.broadcasted_iota(jnp.int32, shape, 0)
        rows = jnp.where(
            which == 0,
            cluster_ref[...] + 1,
            jnp.where(
                which == 1,
                order_row >> 8,
                jnp.where(which == 2, order_row & 255, jnp.where(which == 3, group_row, 0)),
            ),
        ).astype(jnp.float32)
        cols = rows.T
        packed_ref[:, width:] = cols.astype(jnp.bfloat16)
        group_col = cols[:, 3:4]
        above = lax.broadcasted_iota(jnp.int32, (points, points), 0) < lax.broadcasted_iota(
            jnp.int32, (points, points), 1
        )
        same = (group_col == group_row.astype(jnp.float32)) & above
        rank = jnp.sum(same.astype(jnp.float32), axis=0, keepdims=True).astype(jnp.int32)
        group = group_row
        place = rank >> 2
        lane = rank & 3
        dev = place_of(group, place, zs, xs, ys)
        at_prev = place_of(group, (place + 3) & 3, zs, xs, ys) * 12 + 8 + lane
        at_next = place_of(group, (place + 1) & 3, zs, xs, ys) * 12 + 4 + lane
        pick = lax.broadcasted_iota(jnp.int32, idx_ref.shape, 0)
        idx_ref[...] = jnp.where(
            pick == 0,
            dev * 4 + lane,
            jnp.where(pick == 1, dev * 12 + lane, jnp.where(pick == 2, at_prev, at_next)),
        )

    return kernel


def build_send(embeddings, group, point_cluster, point_order, slots, dims, interpret=False):
    points, width = embeddings.shape
    packed, idx = pl.pallas_call(
        prologue(dims),
        out_shape=(
            jax.ShapeDtypeStruct((points, width + EXTRA), jnp.bfloat16),
            jax.ShapeDtypeStruct((8, points), jnp.int32),
        ),
        interpret=interpret,
    )(
        embeddings,
        group.reshape(1, points),
        point_cluster.reshape(1, points),
        point_order.reshape(1, points),
    )
    spot = (idx[0][None, :] == jnp.arange(slots, dtype=jnp.int32)[:, None]).astype(jnp.bfloat16)
    send = lax.dot_general(
        spot, packed, (((1,), (0,)), ((), ())), preferred_element_type=jnp.float32
    ).astype(jnp.bfloat16)
    return send, idx[1:4]


def split_meta(rows, width):
    cluster = rows[:, width].astype(jnp.float32) - 1.0
    order = rows[:, width + 1].astype(jnp.float32) * 256.0 + rows[:, width + 2].astype(jnp.float32)
    return rows[:, :width], cluster, order


def masks(query, keys):
    query_rows, query_cluster, query_order = query
    key_rows, key_cluster, key_order = keys
    scores = lax.dot_general(
        query_rows, key_rows, (((1,), (1,)), ((), ())), preferred_element_type=jnp.float32
    )
    same = query_cluster[:, None] == key_cluster[None, :]
    return scores, same, key_order[None, :] < query_order[:, None]


def best_over(query, keys):
    scores, same, earlier = masks(query, keys)
    return jnp.max(jnp.where(same & earlier, scores, -2.0), axis=1)


def body(embeddings, point_group, point_cluster, point_order, nxt, ring_pos, dims):
    zs, xs, ys = dims
    devices = nxt.shape[0]
    points, width = embeddings.shape
    slots = devices * 4
    group = point_group[:, 0]
    send, idx = build_send(embeddings, group, point_cluster, point_order, slots, dims)
    own = lax.all_to_all(send, ("dp", "blk"), split_axis=0, concat_axis=0, tiled=True)
    forward = [(i, int(nxt[i])) for i in range(devices)]
    backward = [(int(nxt[i]), i) for i in range(devices)]
    prev = lax.ppermute(own, ("dp", "blk"), forward)
    next_ = lax.ppermute(own, ("dp", "blk"), backward)
    query = split_meta(own, width)
    best = best_over(query, query)
    best = jnp.maximum(best, best_over(query, split_meta(prev, width)))
    best = jnp.maximum(best, best_over(query, split_meta(next_, width)))
    half = slots // 2
    me = jnp.asarray(ring_pos)[lax.axis_index(("dp", "blk"))]
    inner = (me == 1) | (me == 2)
    rows = jnp.where(inner, prev[:half], next_[half:])
    cols = jnp.where(inner, next_, prev)
    scores, same_c, earlier = masks(split_meta(rows, width), split_meta(cols, width))
    row_part = jnp.max(jnp.where(same_c & earlier, scores, -2.0), axis=1)
    col_order_r = split_meta(rows, width)[2]
    col_order_c = split_meta(cols, width)[2]
    col_ok = same_c & (col_order_r[:, None] < col_order_c[None, :])
    col_part = jnp.max(jnp.where(col_ok, scores, -2.0), axis=0)
    floor = jnp.full((half,), -2.0, jnp.float32)
    side_prev = jnp.where(inner, jnp.concatenate([row_part, floor]), col_part)
    side_next = jnp.where(inner, col_part, jnp.concatenate([floor, row_part]))
    payload = jnp.stack(
        [best.reshape(devices, 4), side_prev.reshape(devices, 4), side_next.reshape(devices, 4)],
        axis=1,
    ).reshape(devices, 12)
    returned = lax.all_to_all(
        payload, ("dp", "blk"), split_axis=0, concat_axis=0, tiled=True
    ).reshape(devices * 12)
    at_own, at_prev, at_next = idx[0], idx[1], idx[2]
    entry = jnp.arange(devices * 12, dtype=jnp.int32)[None, :]
    pick = (entry == at_own[:, None]) | (entry == at_prev[:, None]) | (entry == at_next[:, None])
    found = jnp.max(jnp.where(pick, returned[None, :], -2.0), axis=1)
    return jnp.where(found > -1.5, found, -1.0)


def solution(mesh):
    dims = (4, 4, 4)
    nxt, ring_pos = ring_of(*dims)
    in_specs = (P(("dp", "blk"), None), P(("dp", "blk"), None), P(("dp", "blk")), P(("dp", "blk")))
    out_specs = P(("dp", "blk"))

    def run(embeddings, point_group, point_cluster, point_order):
        return body(embeddings, point_group, point_cluster, point_order, nxt, ring_pos, dims)

    return jax.shard_map(run, mesh=mesh, in_specs=in_specs, out_specs=out_specs, check_vma=False)
```

```python
import numpy as np
import jax
import jax.numpy as jnp
from jax import lax
from jax.sharding import PartitionSpec as P
from jax.experimental import pallas as pl

EXTRA = 128


def normalize(embeddings):
    values = embeddings.astype(jnp.float32)
    scale = lax.rsqrt(jnp.mean(values * values, axis=1, keepdims=True) + 1e-06)
    width = embeddings.shape[1]
    return (values * scale * width ** (-0.5)).astype(jnp.bfloat16)


def ring_of(zs, xs, ys):
    def lin(z, x, c, y):
        return ((z * xs + x) * 2 + c) * ys + y

    nxt = np.zeros(zs * xs * 2 * ys, np.int32)
    ring_pos = np.zeros(zs * xs * 2 * ys, np.int32)
    for z in range(zs):
        for x in range(xs):
            for y in range(ys):
                nxt[lin(z, x, 0, y)] = lin(z, x, 0, (y + 1) % ys)
                nxt[lin(z, x, 1, y)] = lin(z, (x + 1) % xs, 1, y)
                ring_pos[lin(z, x, 0, y)] = y
                ring_pos[lin(z, x, 1, y)] = x
    return nxt, ring_pos


def device_of(group, place, zs, xs, ys):
    first = group * 2 * ys + place
    other = group - zs * xs
    second = ((other // ys * xs + place) * 2 + 1) * ys + other % ys
    return jnp.where(group < zs * xs, first, second)


def place_of(group, place, zs, xs, ys):
    first = group * 2 * ys + place
    other = group - zs * xs
    second = (((other >> 2) * xs + place) * 2 + 1) * ys + (other & 3)
    return jnp.where(group < zs * xs, first, second)


def prologue(dims):
    zs, xs, ys = dims

    def kernel(emb_ref, group_ref, cluster_ref, order_ref, packed_ref, idx_ref):
        x = emb_ref[...].astype(jnp.float32)
        points, width = x.shape
        scale = lax.rsqrt(jnp.mean(x * x, axis=1, keepdims=True) + 1e-06)
        packed_ref[:, :width] = (x * scale * width ** (-0.5)).astype(jnp.bfloat16)
        group_row = group_ref[...]
        order_row = order_ref[...]
        shape = (packed_ref.shape[1] - width, points)
        which = lax.broadcasted_iota(jnp.int32, shape, 0)
        rows = jnp.where(
            which == 0,
            cluster_ref[...] + 1,
            jnp.where(
                which == 1,
                order_row >> 8,
                jnp.where(which == 2, order_row & 255, jnp.where(which == 3, group_row, 0)),
            ),
        ).astype(jnp.float32)
        cols = rows.T
        packed_ref[:, width:] = cols.astype(jnp.bfloat16)
        group_col = cols[:, 3:4]
        above = lax.broadcasted_iota(jnp.int32, (points, points), 0) < lax.broadcasted_iota(
            jnp.int32, (points, points), 1
        )
        same = (group_col == group_row.astype(jnp.float32)) & above
        rank = jnp.sum(same.astype(jnp.float32), axis=0, keepdims=True).astype(jnp.int32)
        group = group_row
        place = rank >> 2
        lane = rank & 3
        dev = place_of(group, place, zs, xs, ys)
        at_prev = place_of(group, (place + 3) & 3, zs, xs, ys) * 12 + 8 + lane
        at_next = place_of(group, (place + 1) & 3, zs, xs, ys) * 12 + 4 + lane
        pick = lax.broadcasted_iota(jnp.int32, idx_ref.shape, 0)
        idx_ref[...] = jnp.where(
            pick == 0,
            dev * 4 + lane,
            jnp.where(pick == 1, dev * 12 + lane, jnp.where(pick == 2, at_prev, at_next)),
        )

    return kernel


def build_send(embeddings, group, point_cluster, point_order, slots, dims, interpret=False):
    points, width = embeddings.shape
    packed, idx = pl.pallas_call(
        prologue(dims),
        out_shape=(
            jax.ShapeDtypeStruct((points, width + EXTRA), jnp.bfloat16),
            jax.ShapeDtypeStruct((8, points), jnp.int32),
        ),
        interpret=interpret,
    )(
        embeddings,
        group.reshape(1, points),
        point_cluster.reshape(1, points),
        point_order.reshape(1, points),
    )
    spot = (idx[0][None, :] == jnp.arange(slots, dtype=jnp.int32)[:, None]).astype(jnp.bfloat16)
    send = lax.dot_general(
        spot, packed, (((1,), (0,)), ((), ())), preferred_element_type=jnp.float32
    ).astype(jnp.bfloat16)
    return send, idx[1:4]


def split_meta(rows, width):
    cluster = rows[:, width].astype(jnp.float32) - 1.0
    order = rows[:, width + 1].astype(jnp.float32) * 256.0 + rows[:, width + 2].astype(jnp.float32)
    return rows[:, :width], cluster, order


def masks(query, keys):
    query_rows, query_cluster, query_order = query
    key_rows, key_cluster, key_order = keys
    scores = lax.dot_general(
        query_rows, key_rows, (((1,), (1,)), ((), ())), preferred_element_type=jnp.float32
    )
    same = query_cluster[:, None] == key_cluster[None, :]
    return scores, same, key_order[None, :] < query_order[:, None]


def best_over(query, keys):
    scores, same, earlier = masks(query, keys)
    return jnp.max(jnp.where(same & earlier, scores, -2.0), axis=1)


def body(embeddings, point_group, point_cluster, point_order, nxt, ring_pos, dims):
    zs, xs, ys = dims
    devices = nxt.shape[0]
    points, width = embeddings.shape
    slots = devices * 4
    group = point_group[:, 0]
    send, idx = build_send(embeddings, group, point_cluster, point_order, slots, dims)
    own = lax.all_to_all(send, ("dp", "blk"), split_axis=0, concat_axis=0, tiled=True)
    forward = [(i, int(nxt[i])) for i in range(devices)]
    backward = [(int(nxt[i]), i) for i in range(devices)]
    query = split_meta(own, width)
    data = query[0]
    labels = jnp.stack([query[1], query[2]])
    prev_data = lax.ppermute(data, ("dp", "blk"), forward)
    next_data = lax.ppermute(data, ("dp", "blk"), backward)
    prev_labels = lax.ppermute(labels, ("dp", "blk"), forward)
    next_labels = lax.ppermute(labels, ("dp", "blk"), backward)
    prev = (prev_data, prev_labels[0], prev_labels[1])
    next_ = (next_data, next_labels[0], next_labels[1])
    best = best_over(query, query)
    best = jnp.maximum(best, best_over(query, prev))
    best = jnp.maximum(best, best_over(query, next_))
    half = slots // 2
    me = jnp.asarray(ring_pos)[lax.axis_index(("dp", "blk"))]
    inner = (me == 1) | (me == 2)
    rows = tuple(jnp.where(inner, p[:half], n[half:]) for p, n in zip(prev, next_))
    cols = tuple(jnp.where(inner, n, p) for p, n in zip(prev, next_))
    scores, same_c, earlier = masks(rows, cols)
    row_part = jnp.max(jnp.where(same_c & earlier, scores, -2.0), axis=1)
    col_ok = same_c & (rows[2][:, None] < cols[2][None, :])
    col_part = jnp.max(jnp.where(col_ok, scores, -2.0), axis=0)
    floor = jnp.full((half,), -2.0, jnp.float32)
    side_prev = jnp.where(inner, jnp.concatenate([row_part, floor]), col_part)
    side_next = jnp.where(inner, col_part, jnp.concatenate([floor, row_part]))
    payload = jnp.stack(
        [best.reshape(devices, 4), side_prev.reshape(devices, 4), side_next.reshape(devices, 4)],
        axis=1,
    ).reshape(devices, 12)
    returned = lax.all_to_all(
        payload, ("dp", "blk"), split_axis=0, concat_axis=0, tiled=True
    ).reshape(devices * 12)
    at_own, at_prev, at_next = idx[0], idx[1], idx[2]
    entry = jnp.arange(devices * 12, dtype=jnp.int32)[None, :]
    pick = (entry == at_own[:, None]) | (entry == at_prev[:, None]) | (entry == at_next[:, None])
    found = jnp.max(jnp.where(pick, returned[None, :], -2.0), axis=1)
    return jnp.where(found > -1.5, found, -1.0)


def solution(mesh):
    dims = (4, 4, 4)
    nxt, ring_pos = ring_of(*dims)
    in_specs = (P(("dp", "blk"), None), P(("dp", "blk"), None), P(("dp", "blk")), P(("dp", "blk")))
    out_specs = P(("dp", "blk"))

    def run(embeddings, point_group, point_cluster, point_order):
        return body(embeddings, point_group, point_cluster, point_order, nxt, ring_pos, dims)

    return jax.shard_map(run, mesh=mesh, in_specs=in_specs, out_specs=out_specs, check_vma=False)
```

```python
import numpy as np
import jax
import jax.numpy as jnp
from jax import lax
from jax.sharding import PartitionSpec as P
from jax.experimental import pallas as pl

EXTRA = 128


def normalize(embeddings):
    values = embeddings.astype(jnp.float32)
    scale = lax.rsqrt(jnp.mean(values * values, axis=1, keepdims=True) + 1e-06)
    width = embeddings.shape[1]
    return (values * scale * width ** (-0.5)).astype(jnp.bfloat16)


def ring_of(zs, xs, ys):
    def lin(z, x, c, y):
        return ((z * xs + x) * 2 + c) * ys + y

    nxt = np.zeros(zs * xs * 2 * ys, np.int32)
    ring_pos = np.zeros(zs * xs * 2 * ys, np.int32)
    for z in range(zs):
        for x in range(xs):
            for y in range(ys):
                nxt[lin(z, x, 0, y)] = lin(z, x, 0, (y + 1) % ys)
                nxt[lin(z, x, 1, y)] = lin(z, (x + 1) % xs, 1, y)
                ring_pos[lin(z, x, 0, y)] = y
                ring_pos[lin(z, x, 1, y)] = x
    return nxt, ring_pos


def device_of(group, place, zs, xs, ys):
    first = group * 2 * ys + place
    other = group - zs * xs
    second = ((other // ys * xs + place) * 2 + 1) * ys + other % ys
    return jnp.where(group < zs * xs, first, second)


def place_of(group, place, zs, xs, ys):
    first = group * 2 * ys + place
    other = group - zs * xs
    second = (((other >> 2) * xs + place) * 2 + 1) * ys + (other & 3)
    return jnp.where(group < zs * xs, first, second)


def prologue(dims):
    zs, xs, ys = dims

    def kernel(emb_ref, group_ref, cluster_ref, order_ref, packed_ref, target_ref, own_ref, prev_ref, next_ref):
        x = emb_ref[...].astype(jnp.float32)
        points, width = x.shape
        scale = lax.rsqrt(jnp.mean(x * x, axis=1, keepdims=True) + 1e-06)
        packed_ref[:, :width] = (x * scale * width ** (-0.5)).astype(jnp.bfloat16)
        group_row = group_ref[...]
        order_row = order_ref[...]
        shape = (packed_ref.shape[1] - width, points)
        which = lax.broadcasted_iota(jnp.int32, shape, 0)
        rows = jnp.where(
            which == 0,
            cluster_ref[...] + 1,
            jnp.where(
                which == 1,
                order_row >> 8,
                jnp.where(which == 2, order_row & 255, jnp.where(which == 3, group_row, 0)),
            ),
        ).astype(jnp.float32)
        cols = rows.T
        packed_ref[:, width:] = cols.astype(jnp.bfloat16)
        group_col = cols[:, 3:4]
        above = lax.broadcasted_iota(jnp.int32, (points, points), 0) < lax.broadcasted_iota(
            jnp.int32, (points, points), 1
        )
        same = (group_col == group_row.astype(jnp.float32)) & above
        rank = jnp.sum(same.astype(jnp.float32), axis=0, keepdims=True).astype(jnp.int32)
        group = group_row
        place = rank >> 2
        lane = rank & 3
        dev = place_of(group, place, zs, xs, ys)
        at_prev = place_of(group, (place + 3) & 3, zs, xs, ys) * 12 + 8 + lane
        at_next = place_of(group, (place + 1) & 3, zs, xs, ys) * 12 + 4 + lane
        target_ref[...] = dev * 4 + lane
        own_ref[...] = dev * 12 + lane
        prev_ref[...] = at_prev
        next_ref[...] = at_next

    return kernel


def build_send(embeddings, group, point_cluster, point_order, slots, dims, interpret=False):
    points, width = embeddings.shape
    packed, target, at_own, at_prev, at_next = pl.pallas_call(
        prologue(dims),
        out_shape=(jax.ShapeDtypeStruct((points, width + EXTRA), jnp.bfloat16),)
        + tuple(jax.ShapeDtypeStruct((1, points), jnp.int32) for _ in range(4)),
        interpret=interpret,
    )(
        embeddings,
        group.reshape(1, points),
        point_cluster.reshape(1, points),
        point_order.reshape(1, points),
    )
    spot = (target.reshape(points)[None, :] == jnp.arange(slots, dtype=jnp.int32)[:, None]).astype(jnp.bfloat16)
    send = lax.dot_general(
        spot, packed, (((1,), (0,)), ((), ())), preferred_element_type=jnp.float32
    ).astype(jnp.bfloat16)
    return send, tuple(a.reshape(points) for a in (at_own, at_prev, at_next))


def split_meta(rows, width):
    cluster = rows[:, width].astype(jnp.float32) - 1.0
    order = rows[:, width + 1].astype(jnp.float32) * 256.0 + rows[:, width + 2].astype(jnp.float32)
    return rows[:, :width], cluster, order


def masks(query, keys):
    query_rows, query_cluster, query_order = query
    key_rows, key_cluster, key_order = keys
    scores = lax.dot_general(
        query_rows, key_rows, (((1,), (1,)), ((), ())), preferred_element_type=jnp.float32
    )
    same = query_cluster[:, None] == key_cluster[None, :]
    return scores, same, key_order[None, :] < query_order[:, None]


def best_over(query, keys):
    scores, same, earlier = masks(query, keys)
    return jnp.max(jnp.where(same & earlier, scores, -2.0), axis=1)


def body(embeddings, point_group, point_cluster, point_order, nxt, ring_pos, dims):
    zs, xs, ys = dims
    devices = nxt.shape[0]
    points, width = embeddings.shape
    slots = devices * 4
    group = point_group[:, 0]
    send, idx = build_send(embeddings, group, point_cluster, point_order, slots, dims)
    own = lax.all_to_all(send, ("dp", "blk"), split_axis=0, concat_axis=0, tiled=True)
    forward = [(i, int(nxt[i])) for i in range(devices)]
    backward = [(int(nxt[i]), i) for i in range(devices)]
    query = split_meta(own, width)
    data = query[0]
    labels = jnp.stack([query[1], query[2]])
    prev_data = lax.ppermute(data, ("dp", "blk"), forward)
    next_data = lax.ppermute(data, ("dp", "blk"), backward)
    prev_labels = lax.ppermute(labels, ("dp", "blk"), forward)
    next_labels = lax.ppermute(labels, ("dp", "blk"), backward)
    prev = (prev_data, prev_labels[0], prev_labels[1])
    next_ = (next_data, next_labels[0], next_labels[1])
    best = best_over(query, query)
    best = jnp.maximum(best, best_over(query, prev))
    best = jnp.maximum(best, best_over(query, next_))
    half = slots // 2
    me = jnp.asarray(ring_pos)[lax.axis_index(("dp", "blk"))]
    inner = (me == 1) | (me == 2)
    rows = tuple(jnp.where(inner, p[:half], n[half:]) for p, n in zip(prev, next_))
    cols = tuple(jnp.where(inner, n, p) for p, n in zip(prev, next_))
    scores, same_c, earlier = masks(rows, cols)
    row_part = jnp.max(jnp.where(same_c & earlier, scores, -2.0), axis=1)
    col_ok = same_c & (rows[2][:, None] < cols[2][None, :])
    col_part = jnp.max(jnp.where(col_ok, scores, -2.0), axis=0)
    floor = jnp.full((half,), -2.0, jnp.float32)
    side_prev = jnp.where(inner, jnp.concatenate([row_part, floor]), col_part)
    side_next = jnp.where(inner, col_part, jnp.concatenate([floor, row_part]))
    payload = jnp.concatenate(
        [v.reshape(devices, 1, 4) for v in (best, side_prev, side_next)], axis=2
    )
    returned = lax.all_to_all(
        payload, ("dp", "blk"), split_axis=0, concat_axis=0, tiled=False
    ).reshape(devices * 12)
    at_own, at_prev, at_next = idx[0], idx[1], idx[2]
    entry = jnp.arange(devices * 12, dtype=jnp.int32)[None, :]
    pick = (entry == at_own[:, None]) | (entry == at_prev[:, None]) | (entry == at_next[:, None])
    found = jnp.max(jnp.where(pick, returned[None, :], -2.0), axis=1)
    return jnp.where(found > -1.5, found, -1.0)


def solution(mesh):
    dims = (4, 4, 4)
    nxt, ring_pos = ring_of(*dims)
    in_specs = (P(("dp", "blk"), None), P(("dp", "blk"), None), P(("dp", "blk")), P(("dp", "blk")))
    out_specs = P(("dp", "blk"))

    def run(embeddings, point_group, point_cluster, point_order):
        return body(embeddings, point_group, point_cluster, point_order, nxt, ring_pos, dims)

    return jax.shard_map(run, mesh=mesh, in_specs=in_specs, out_specs=out_specs, check_vma=False)
```

```python
import numpy as np
import jax
import jax.numpy as jnp
from jax import lax
from jax.sharding import PartitionSpec as P
from jax.experimental import pallas as pl

EXTRA = 128


def normalize(embeddings):
    values = embeddings.astype(jnp.float32)
    scale = lax.rsqrt(jnp.mean(values * values, axis=1, keepdims=True) + 1e-06)
    width = embeddings.shape[1]
    return (values * scale * width ** (-0.5)).astype(jnp.bfloat16)


def ring_of(zs, xs, ys):
    def lin(z, x, c, y):
        return ((z * xs + x) * 2 + c) * ys + y

    nxt = np.zeros(zs * xs * 2 * ys, np.int32)
    ring_pos = np.zeros(zs * xs * 2 * ys, np.int32)
    for z in range(zs):
        for x in range(xs):
            for y in range(ys):
                nxt[lin(z, x, 0, y)] = lin(z, x, 0, (y + 1) % ys)
                nxt[lin(z, x, 1, y)] = lin(z, (x + 1) % xs, 1, y)
                ring_pos[lin(z, x, 0, y)] = y
                ring_pos[lin(z, x, 1, y)] = x
    return nxt, ring_pos


def device_of(group, place, zs, xs, ys):
    first = group * 2 * ys + place
    other = group - zs * xs
    second = ((other // ys * xs + place) * 2 + 1) * ys + other % ys
    return jnp.where(group < zs * xs, first, second)


def place_of(group, place, zs, xs, ys):
    first = group * 2 * ys + place
    other = group - zs * xs
    second = (((other >> 2) * xs + place) * 2 + 1) * ys + (other & 3)
    return jnp.where(group < zs * xs, first, second)


def prologue(dims):
    zs, xs, ys = dims

    def kernel(emb_ref, group_ref, cluster_ref, order_ref, packed_ref, target_ref, own_ref, prev_ref, next_ref):
        x = emb_ref[...].astype(jnp.float32)
        points, width = x.shape
        scale = lax.rsqrt(jnp.mean(x * x, axis=1, keepdims=True) + 1e-06)
        packed_ref[:, :width] = (x * scale * width ** (-0.5)).astype(jnp.bfloat16)
        group_row = group_ref[...]
        order_row = order_ref[...]
        shape = (packed_ref.shape[1] - width, points)
        which = lax.broadcasted_iota(jnp.int32, shape, 0)
        rows = jnp.where(
            which == 0,
            cluster_ref[...] + 1,
            jnp.where(
                which == 1,
                order_row >> 8,
                jnp.where(which == 2, order_row & 255, jnp.where(which == 3, group_row, 0)),
            ),
        ).astype(jnp.float32)
        cols = rows.T
        packed_ref[:, width:] = cols.astype(jnp.bfloat16)
        group_col = cols[:, 3:4]
        above = lax.broadcasted_iota(jnp.int32, (points, points), 0) < lax.broadcasted_iota(
            jnp.int32, (points, points), 1
        )
        same = (group_col == group_row.astype(jnp.float32)) & above
        rank = jnp.sum(same.astype(jnp.float32), axis=0, keepdims=True).astype(jnp.int32)
        group = group_row
        place = rank >> 2
        lane = rank & 3
        dev = place_of(group, place, zs, xs, ys)
        at_prev = place_of(group, (place + 3) & 3, zs, xs, ys) * 12 + 8 + lane
        at_next = place_of(group, (place + 1) & 3, zs, xs, ys) * 12 + 4 + lane
        target_ref[...] = dev * 4 + lane
        own_ref[...] = dev * 12 + lane
        prev_ref[...] = at_prev
        next_ref[...] = at_next

    return kernel


def build_send(embeddings, group, point_cluster, point_order, slots, dims, interpret=False):
    points, width = embeddings.shape
    packed, target, at_own, at_prev, at_next = pl.pallas_call(
        prologue(dims),
        out_shape=(jax.ShapeDtypeStruct((points, width + EXTRA), jnp.bfloat16),)
        + tuple(jax.ShapeDtypeStruct((1, points), jnp.int32) for _ in range(4)),
        interpret=interpret,
    )(
        embeddings,
        group.reshape(1, points),
        point_cluster.reshape(1, points),
        point_order.reshape(1, points),
    )
    spot = (target.reshape(points)[None, :] == jnp.arange(slots, dtype=jnp.int32)[:, None]).astype(jnp.bfloat16)
    send = lax.dot_general(
        spot, packed, (((1,), (0,)), ((), ())), preferred_element_type=jnp.float32
    ).astype(jnp.bfloat16)
    return send, tuple(a.reshape(points) for a in (at_own, at_prev, at_next))


def split_meta(rows, width):
    cluster = rows[:, width].astype(jnp.float32) - 1.0
    order = rows[:, width + 1].astype(jnp.float32) * 256.0 + rows[:, width + 2].astype(jnp.float32)
    return rows[:, :width], cluster, order


def unpack(ring, slots):
    marks = ring[slots:].reshape(-1).astype(jnp.float32)
    cluster = marks[:slots] - 1.0
    order = marks[slots : 2 * slots] * 256.0 + marks[2 * slots : 3 * slots]
    return ring[:slots], cluster, order


def masks(query, keys):
    query_rows, query_cluster, query_order = query
    key_rows, key_cluster, key_order = keys
    scores = lax.dot_general(
        query_rows, key_rows, (((1,), (1,)), ((), ())), preferred_element_type=jnp.float32
    )
    same = query_cluster[:, None] == key_cluster[None, :]
    return scores, same, key_order[None, :] < query_order[:, None]


def best_over(query, keys):
    scores, same, earlier = masks(query, keys)
    return jnp.max(jnp.where(same & earlier, scores, -2.0), axis=1)


def body(embeddings, point_group, point_cluster, point_order, nxt, ring_pos, dims):
    zs, xs, ys = dims
    devices = nxt.shape[0]
    points, width = embeddings.shape
    slots = devices * 4
    group = point_group[:, 0]
    send, idx = build_send(embeddings, group, point_cluster, point_order, slots, dims)
    own = lax.all_to_all(send, ("dp", "blk"), split_axis=0, concat_axis=0, tiled=True)
    forward = [(i, int(nxt[i])) for i in range(devices)]
    backward = [(int(nxt[i]), i) for i in range(devices)]
    query = split_meta(own, width)
    marks = jnp.concatenate([own[:, width + k] for k in range(3)]).reshape(-1, width)
    ring = jnp.concatenate([query[0], marks], axis=0)
    prev = unpack(lax.ppermute(ring, ("dp", "blk"), forward), slots)
    next_ = unpack(lax.ppermute(ring, ("dp", "blk"), backward), slots)
    best = best_over(query, query)
    best = jnp.maximum(best, best_over(query, prev))
    best = jnp.maximum(best, best_over(query, next_))
    half = slots // 2
    me = jnp.asarray(ring_pos)[lax.axis_index(("dp", "blk"))]
    inner = (me == 1) | (me == 2)
    rows = tuple(jnp.where(inner, p[:half], n[half:]) for p, n in zip(prev, next_))
    cols = tuple(jnp.where(inner, n, p) for p, n in zip(prev, next_))
    scores, same_c, earlier = masks(rows, cols)
    row_part = jnp.max(jnp.where(same_c & earlier, scores, -2.0), axis=1)
    col_ok = same_c & (rows[2][:, None] < cols[2][None, :])
    col_part = jnp.max(jnp.where(col_ok, scores, -2.0), axis=0)
    floor = jnp.full((half,), -2.0, jnp.float32)
    side_prev = jnp.where(inner, jnp.concatenate([row_part, floor]), col_part)
    side_next = jnp.where(inner, col_part, jnp.concatenate([floor, row_part]))
    payload = jnp.concatenate(
        [v.reshape(devices, 1, 4) for v in (best, side_prev, side_next)], axis=2
    )
    returned = lax.all_to_all(
        payload, ("dp", "blk"), split_axis=0, concat_axis=0, tiled=False
    ).reshape(devices * 12)
    at_own, at_prev, at_next = idx[0], idx[1], idx[2]
    entry = jnp.arange(devices * 12, dtype=jnp.int32)[None, :]
    pick = (entry == at_own[:, None]) | (entry == at_prev[:, None]) | (entry == at_next[:, None])
    found = jnp.max(jnp.where(pick, returned[None, :], -2.0), axis=1)
    return jnp.where(found > -1.5, found, -1.0)


def solution(mesh):
    dims = (4, 4, 4)
    nxt, ring_pos = ring_of(*dims)
    in_specs = (P(("dp", "blk"), None), P(("dp", "blk"), None), P(("dp", "blk")), P(("dp", "blk")))
    out_specs = P(("dp", "blk"))

    def run(embeddings, point_group, point_cluster, point_order):
        return body(embeddings, point_group, point_cluster, point_order, nxt, ring_pos, dims)

    return jax.shard_map(run, mesh=mesh, in_specs=in_specs, out_specs=out_specs, check_vma=False)
```

```python
import numpy as np
import jax
import jax.numpy as jnp
from jax import lax
from jax.sharding import PartitionSpec as P
from jax.experimental import pallas as pl

EXTRA = 128


def ring_of(zs, xs, ys):
    def lin(z, x, c, y):
        return ((z * xs + x) * 2 + c) * ys + y

    nxt = np.zeros(zs * xs * 2 * ys, np.int32)
    ring_pos = np.zeros(zs * xs * 2 * ys, np.int32)
    for z in range(zs):
        for x in range(xs):
            for y in range(ys):
                nxt[lin(z, x, 0, y)] = lin(z, x, 0, (y + 1) % ys)
                nxt[lin(z, x, 1, y)] = lin(z, (x + 1) % xs, 1, y)
                ring_pos[lin(z, x, 0, y)] = y
                ring_pos[lin(z, x, 1, y)] = x
    return nxt, ring_pos


def place_of(group, place, zs, xs, ys):
    first = group * 2 * ys + place
    other = group - zs * xs
    second = (((other >> 2) * xs + place) * 2 + 1) * ys + (other & 3)
    return jnp.where(group < zs * xs, first, second)


def prologue(dims):
    zs, xs, ys = dims

    def kernel(emb_ref, group_ref, cluster_ref, order_ref, packed_ref, target_ref, own_ref, prev_ref, next_ref):
        x = emb_ref[...].astype(jnp.float32)
        points, width = x.shape
        scale = lax.rsqrt(jnp.mean(x * x, axis=1, keepdims=True) + 1e-06)
        packed_ref[:, :width] = (x * scale * width ** (-0.5)).astype(jnp.bfloat16)
        group_row = group_ref[...]
        order_row = order_ref[...]
        shape = (packed_ref.shape[1] - width, points)
        which = lax.broadcasted_iota(jnp.int32, shape, 0)
        rows = jnp.where(
            which == 0,
            cluster_ref[...] + 1,
            jnp.where(
                which == 1,
                order_row >> 8,
                jnp.where(which == 2, order_row & 255, jnp.where(which == 3, group_row, 0)),
            ),
        ).astype(jnp.float32)
        cols = rows.T
        packed_ref[:, width:] = cols.astype(jnp.bfloat16)
        group_col = cols[:, 3:4]
        above = lax.broadcasted_iota(jnp.int32, (points, points), 0) < lax.broadcasted_iota(
            jnp.int32, (points, points), 1
        )
        same = (group_col == group_row.astype(jnp.float32)) & above
        rank = jnp.sum(same.astype(jnp.float32), axis=0, keepdims=True).astype(jnp.int32)
        group = group_row
        place = rank >> 2
        lane = rank & 3
        dev = place_of(group, place, zs, xs, ys)
        at_prev = place_of(group, (place + 3) & 3, zs, xs, ys) * 12 + 8 + lane
        at_next = place_of(group, (place + 1) & 3, zs, xs, ys) * 12 + 4 + lane
        target_ref[...] = dev * 4 + lane
        own_ref[...] = dev * 12 + lane
        prev_ref[...] = at_prev
        next_ref[...] = at_next

    return kernel


def build_send(embeddings, group, point_cluster, point_order, slots, dims, interpret=False):
    points, width = embeddings.shape
    packed, target, at_own, at_prev, at_next = pl.pallas_call(
        prologue(dims),
        out_shape=(jax.ShapeDtypeStruct((points, width + EXTRA), jnp.bfloat16),)
        + tuple(jax.ShapeDtypeStruct((1, points), jnp.int32) for _ in range(4)),
        interpret=interpret,
    )(
        embeddings,
        group.reshape(1, points),
        point_cluster.reshape(1, points),
        point_order.reshape(1, points),
    )
    spot = (target.reshape(points)[None, :] == jnp.arange(slots, dtype=jnp.int32)[:, None]).astype(jnp.bfloat16)
    send = lax.dot_general(
        spot, packed, (((1,), (0,)), ((), ())), preferred_element_type=jnp.float32
    ).astype(jnp.bfloat16)
    return send, tuple(a.reshape(points) for a in (at_own, at_prev, at_next))


def split_meta(rows, width):
    cluster = rows[:, width].astype(jnp.float32) - 1.0
    order = rows[:, width + 1].astype(jnp.float32) * 256.0 + rows[:, width + 2].astype(jnp.float32)
    return rows[:, :width], cluster, order


def masks(query, keys):
    query_rows, query_cluster, query_order = query
    key_rows, key_cluster, key_order = keys
    scores = lax.dot_general(
        query_rows, key_rows, (((1,), (1,)), ((), ())), preferred_element_type=jnp.float32
    )
    same = query_cluster[:, None] == key_cluster[None, :]
    return scores, same, key_order[None, :] < query_order[:, None]


def best_over(query, keys):
    scores, same, earlier = masks(query, keys)
    return jnp.max(jnp.where(same & earlier, scores, -2.0), axis=1)


def body(embeddings, point_group, point_cluster, point_order, nxt, ring_pos, dims):
    devices = nxt.shape[0]
    _, width = embeddings.shape
    slots = devices * 4
    group = point_group[:, 0]
    send, idx = build_send(embeddings, group, point_cluster, point_order, slots, dims)
    own = lax.all_to_all(send, ("dp", "blk"), split_axis=0, concat_axis=0, tiled=True)
    forward = [(i, int(nxt[i])) for i in range(devices)]
    backward = [(int(nxt[i]), i) for i in range(devices)]
    query = split_meta(own, width)
    data = query[0]
    labels = jnp.stack([query[1], query[2]])
    prev_labels = lax.ppermute(labels, ("dp", "blk"), forward)
    next_labels = lax.ppermute(labels, ("dp", "blk"), backward)
    prev_data = lax.ppermute(data, ("dp", "blk"), forward)
    next_data = lax.ppermute(data, ("dp", "blk"), backward)
    prev = (prev_data, prev_labels[0], prev_labels[1])
    next_ = (next_data, next_labels[0], next_labels[1])
    best = best_over(query, query)
    best = jnp.maximum(best, best_over(query, prev))
    best = jnp.maximum(best, best_over(query, next_))
    half = slots // 2
    me = jnp.asarray(ring_pos)[lax.axis_index(("dp", "blk"))]
    inner = (me == 1) | (me == 2)
    rows = tuple(jnp.where(inner, p[:half], n[half:]) for p, n in zip(prev, next_))
    cols = tuple(jnp.where(inner, n, p) for p, n in zip(prev, next_))
    scores, same_c, earlier = masks(rows, cols)
    row_part = jnp.max(jnp.where(same_c & earlier, scores, -2.0), axis=1)
    col_ok = same_c & (rows[2][:, None] < cols[2][None, :])
    col_part = jnp.max(jnp.where(col_ok, scores, -2.0), axis=0)
    floor = jnp.full((half,), -2.0, jnp.float32)
    side_prev = jnp.where(inner, jnp.concatenate([row_part, floor]), col_part)
    side_next = jnp.where(inner, col_part, jnp.concatenate([floor, row_part]))
    payload = jnp.concatenate(
        [v.reshape(devices, 1, 4) for v in (best, side_prev, side_next)], axis=2
    )
    returned = lax.all_to_all(
        payload, ("dp", "blk"), split_axis=0, concat_axis=0, tiled=False
    ).reshape(devices * 12)
    at_own, at_prev, at_next = idx[0], idx[1], idx[2]
    entry = jnp.arange(devices * 12, dtype=jnp.int32)[None, :]
    pick = (entry == at_own[:, None]) | (entry == at_prev[:, None]) | (entry == at_next[:, None])
    found = jnp.max(jnp.where(pick, returned[None, :], -2.0), axis=1)
    return jnp.where(found > -1.5, found, -1.0)


def solution(mesh):
    dims = (4, 4, 4)
    nxt, ring_pos = ring_of(*dims)
    in_specs = (P(("dp", "blk"), None), P(("dp", "blk"), None), P(("dp", "blk")), P(("dp", "blk")))
    out_specs = P(("dp", "blk"))

    def run(embeddings, point_group, point_cluster, point_order):
        return body(embeddings, point_group, point_cluster, point_order, nxt, ring_pos, dims)

    return jax.shard_map(run, mesh=mesh, in_specs=in_specs, out_specs=out_specs, check_vma=False)
```

```python
import numpy as np
import jax
import jax.numpy as jnp
from jax import lax
from jax.sharding import PartitionSpec as P
from jax.experimental import pallas as pl

EXTRA = 128


def ring_of(zs, xs, ys):
    def lin(z, x, c, y):
        return ((z * xs + x) * 2 + c) * ys + y

    nxt = np.zeros(zs * xs * 2 * ys, np.int32)
    ring_pos = np.zeros(zs * xs * 2 * ys, np.int32)
    for z in range(zs):
        for x in range(xs):
            for y in range(ys):
                nxt[lin(z, x, 0, y)] = lin(z, x, 0, (y + 1) % ys)
                nxt[lin(z, x, 1, y)] = lin(z, (x + 1) % xs, 1, y)
                ring_pos[lin(z, x, 0, y)] = y
                ring_pos[lin(z, x, 1, y)] = x
    return nxt, ring_pos


def place_of(group, place, zs, xs, ys):
    first = group * 2 * ys + place
    other = group - zs * xs
    second = (((other >> 2) * xs + place) * 2 + 1) * ys + (other & 3)
    return jnp.where(group < zs * xs, first, second)


def prologue(dims):
    zs, xs, ys = dims

    def kernel(emb_ref, group_ref, cluster_ref, order_ref, packed_ref, target_ref, own_ref, prev_ref, next_ref):
        x = emb_ref[...].astype(jnp.float32)
        points, width = x.shape
        scale = lax.rsqrt(jnp.mean(x * x, axis=1, keepdims=True) + 1e-06)
        packed_ref[:, :width] = (x * scale * width ** (-0.5)).astype(jnp.bfloat16)
        group_row = group_ref[...]
        order_row = order_ref[...]
        shape = (packed_ref.shape[1] - width, points)
        which = lax.broadcasted_iota(jnp.int32, shape, 0)
        rows = jnp.where(
            which == 0,
            cluster_ref[...] + 1,
            jnp.where(
                which == 1,
                order_row >> 8,
                jnp.where(which == 2, order_row & 255, jnp.where(which == 3, group_row, 0)),
            ),
        ).astype(jnp.float32)
        cols = rows.T
        packed_ref[:, width:] = cols.astype(jnp.bfloat16)
        group_col = cols[:, 3:4]
        above = lax.broadcasted_iota(jnp.int32, (points, points), 0) < lax.broadcasted_iota(
            jnp.int32, (points, points), 1
        )
        same = (group_col == group_row.astype(jnp.float32)) & above
        rank = jnp.sum(same.astype(jnp.float32), axis=0, keepdims=True).astype(jnp.int32)
        group = group_row
        place = rank >> 2
        lane = rank & 3
        dev = place_of(group, place, zs, xs, ys)
        at_prev = place_of(group, (place + 3) & 3, zs, xs, ys) * 12 + 8 + lane
        at_next = place_of(group, (place + 1) & 3, zs, xs, ys) * 12 + 4 + lane
        target_ref[...] = dev * 4 + lane
        own_ref[...] = dev * 12 + lane
        prev_ref[...] = at_prev
        next_ref[...] = at_next

    return kernel


def build_send(embeddings, group, point_cluster, point_order, slots, dims, interpret=False):
    points, width = embeddings.shape
    packed, target, at_own, at_prev, at_next = pl.pallas_call(
        prologue(dims),
        out_shape=(jax.ShapeDtypeStruct((points, width + EXTRA), jnp.bfloat16),)
        + tuple(jax.ShapeDtypeStruct((1, points), jnp.int32) for _ in range(4)),
        interpret=interpret,
    )(
        embeddings,
        group.reshape(1, points),
        point_cluster.reshape(1, points),
        point_order.reshape(1, points),
    )
    spot = (target.reshape(points)[None, :] == jnp.arange(slots, dtype=jnp.int32)[:, None]).astype(jnp.bfloat16)
    send = lax.dot_general(
        spot, packed, (((1,), (0,)), ((), ())), preferred_element_type=jnp.float32
    ).astype(jnp.bfloat16)
    return send, tuple(a.reshape(points) for a in (at_own, at_prev, at_next))


def split_meta(rows, width):
    cluster = rows[:, width].astype(jnp.float32) - 1.0
    order = rows[:, width + 1].astype(jnp.float32) * 256.0 + rows[:, width + 2].astype(jnp.float32)
    return rows[:, :width], cluster, order


def masks(query, keys):
    query_rows, query_cluster, query_order = query
    key_rows, key_cluster, key_order = keys
    scores = lax.dot_general(
        query_rows, key_rows, (((1,), (1,)), ((), ())), preferred_element_type=jnp.float32
    )
    same = query_cluster[:, None] == key_cluster[None, :]
    return scores, same, key_order[None, :] < query_order[:, None]


def best_over(query, keys):
    scores, same, earlier = masks(query, keys)
    return jnp.max(jnp.where(same & earlier, scores, -2.0), axis=1)


def body(embeddings, point_group, point_cluster, point_order, nxt, dims):
    _, xs, ys = dims
    devices = nxt.shape[0]
    _, width = embeddings.shape
    slots = devices * 4
    group = point_group[:, 0]
    send, idx = build_send(embeddings, group, point_cluster, point_order, slots, dims)
    own = lax.all_to_all(send, ("dp", "blk"), split_axis=0, concat_axis=0, tiled=True)
    forward = [(i, int(nxt[i])) for i in range(devices)]
    backward = [(int(nxt[i]), i) for i in range(devices)]
    query = split_meta(own, width)
    data = query[0]
    labels = jnp.stack([query[1], query[2]])
    prev_data = lax.ppermute(data, ("dp", "blk"), forward)
    next_data = lax.ppermute(data, ("dp", "blk"), backward)
    prev_labels = lax.ppermute(labels, ("dp", "blk"), forward)
    next_labels = lax.ppermute(labels, ("dp", "blk"), backward)
    prev = (prev_data, prev_labels[0], prev_labels[1])
    next_ = (next_data, next_labels[0], next_labels[1])
    best = best_over(query, query)
    best = jnp.maximum(best, best_over(query, prev))
    best = jnp.maximum(best, best_over(query, next_))
    half = slots // 2
    here = lax.axis_index(("dp", "blk"))
    me = jnp.where((here // ys) % 2 == 0, here % ys, (here // (2 * ys)) % xs)
    inner = (me == 1) | (me == 2)
    rows = tuple(jnp.where(inner, p[:half], n[half:]) for p, n in zip(prev, next_))
    cols = tuple(jnp.where(inner, n, p) for p, n in zip(prev, next_))
    scores, same_c, earlier = masks(rows, cols)
    row_part = jnp.max(jnp.where(same_c & earlier, scores, -2.0), axis=1)
    col_ok = same_c & (rows[2][:, None] < cols[2][None, :])
    col_part = jnp.max(jnp.where(col_ok, scores, -2.0), axis=0)
    floor = jnp.full((half,), -2.0, jnp.float32)
    side_prev = jnp.where(inner, jnp.concatenate([row_part, floor]), col_part)
    side_next = jnp.where(inner, col_part, jnp.concatenate([floor, row_part]))
    payload = jnp.concatenate(
        [v.reshape(devices, 1, 4) for v in (best, side_prev, side_next)], axis=2
    )
    returned = lax.all_to_all(
        payload, ("dp", "blk"), split_axis=0, concat_axis=0, tiled=False
    ).reshape(devices * 12)
    at_own, at_prev, at_next = idx[0], idx[1], idx[2]
    entry = jnp.arange(devices * 12, dtype=jnp.int32)[None, :]
    pick = (entry == at_own[:, None]) | (entry == at_prev[:, None]) | (entry == at_next[:, None])
    found = jnp.max(jnp.where(pick, returned[None, :], -2.0), axis=1)
    return jnp.where(found > -1.5, found, -1.0)


def solution(mesh):
    dims = (4, 4, 4)
    nxt, _ = ring_of(*dims)
    in_specs = (P(("dp", "blk"), None), P(("dp", "blk"), None), P(("dp", "blk")), P(("dp", "blk")))
    out_specs = P(("dp", "blk"))

    def run(embeddings, point_group, point_cluster, point_order):
        return body(embeddings, point_group, point_cluster, point_order, nxt, dims)

    return jax.shard_map(run, mesh=mesh, in_specs=in_specs, out_specs=out_specs, check_vma=False)
```

```python
import numpy as np
import jax
import jax.numpy as jnp
from jax import lax
from jax.sharding import PartitionSpec as P
from jax.experimental import pallas as pl

EXTRA = 128


def ring_of(zs, xs, ys):
    def lin(z, x, c, y):
        return ((z * xs + x) * 2 + c) * ys + y

    nxt = np.zeros(zs * xs * 2 * ys, np.int32)
    ring_pos = np.zeros(zs * xs * 2 * ys, np.int32)
    for z in range(zs):
        for x in range(xs):
            for y in range(ys):
                nxt[lin(z, x, 0, y)] = lin(z, x, 0, (y + 1) % ys)
                nxt[lin(z, x, 1, y)] = lin(z, (x + 1) % xs, 1, y)
                ring_pos[lin(z, x, 0, y)] = y
                ring_pos[lin(z, x, 1, y)] = x
    return nxt, ring_pos


def place_of(group, place, zs, xs, ys):
    first = group * 2 * ys + place
    other = group - zs * xs
    second = (((other >> 2) * xs + place) * 2 + 1) * ys + (other & 3)
    return jnp.where(group < zs * xs, first, second)


def prologue(dims):
    zs, xs, ys = dims

    def kernel(emb_ref, group_ref, cluster_ref, order_ref, packed_ref, target_ref, own_ref, prev_ref, next_ref):
        x = emb_ref[...].astype(jnp.float32)
        points, width = x.shape
        scale = lax.rsqrt(jnp.mean(x * x, axis=1, keepdims=True) + 1e-06)
        packed_ref[:, :width] = (x * scale * width ** (-0.5)).astype(jnp.bfloat16)
        group_row = group_ref[...]
        order_row = order_ref[...]
        shape = (packed_ref.shape[1] - width, points)
        which = lax.broadcasted_iota(jnp.int32, shape, 0)
        rows = jnp.where(
            which == 0,
            cluster_ref[...] + 1,
            jnp.where(
                which == 1,
                order_row >> 8,
                jnp.where(which == 2, order_row & 255, jnp.where(which == 3, group_row, 0)),
            ),
        ).astype(jnp.float32)
        cols = rows.T
        packed_ref[:, width:] = cols.astype(jnp.bfloat16)
        group_col = cols[:, 3:4]
        above = lax.broadcasted_iota(jnp.int32, (points, points), 0) < lax.broadcasted_iota(
            jnp.int32, (points, points), 1
        )
        same = (group_col == group_row.astype(jnp.float32)) & above
        rank = jnp.sum(same.astype(jnp.float32), axis=0, keepdims=True).astype(jnp.int32)
        group = group_row
        place = rank >> 2
        lane = rank & 3
        dev = place_of(group, place, zs, xs, ys)
        at_prev = place_of(group, (place + 3) & 3, zs, xs, ys) * 12 + 8 + lane
        at_next = place_of(group, (place + 1) & 3, zs, xs, ys) * 12 + 4 + lane
        target_ref[...] = dev * 4 + lane
        own_ref[...] = dev * 12 + lane
        prev_ref[...] = at_prev
        next_ref[...] = at_next

    return kernel


def build_send(embeddings, group, point_cluster, point_order, slots, dims, interpret=False):
    points, width = embeddings.shape
    packed, target, at_own, at_prev, at_next = pl.pallas_call(
        prologue(dims),
        out_shape=(jax.ShapeDtypeStruct((points, width + EXTRA), jnp.bfloat16),)
        + tuple(jax.ShapeDtypeStruct((1, points), jnp.int32) for _ in range(4)),
        interpret=interpret,
    )(
        embeddings,
        group.reshape(1, points),
        point_cluster.reshape(1, points),
        point_order.reshape(1, points),
    )
    spot = (target.reshape(points)[None, :] == jnp.arange(slots, dtype=jnp.int32)[:, None]).astype(jnp.bfloat16)
    send = lax.dot_general(
        spot, packed, (((1,), (0,)), ((), ())), preferred_element_type=jnp.float32
    ).astype(jnp.bfloat16)
    return send, tuple(a.reshape(points) for a in (at_own, at_prev, at_next))


def split_meta(rows, width):
    cluster = rows[:, width].astype(jnp.float32) - 1.0
    order = rows[:, width + 1].astype(jnp.float32) * 256.0 + rows[:, width + 2].astype(jnp.float32)
    return rows[:, :width], cluster, order


def masks(query, keys):
    query_rows, query_cluster, query_order = query
    key_rows, key_cluster, key_order = keys
    scores = lax.dot_general(
        query_rows, key_rows, (((1,), (1,)), ((), ())), preferred_element_type=jnp.float32
    )
    same = query_cluster[:, None] == key_cluster[None, :]
    return scores, same, key_order[None, :] < query_order[:, None]


def best_over(query, keys):
    scores, same, earlier = masks(query, keys)
    return jnp.max(jnp.where(same & earlier, scores, -2.0), axis=1)


def body(embeddings, point_group, point_cluster, point_order, nxt, dims):
    _, xs, ys = dims
    devices = nxt.shape[0]
    _, width = embeddings.shape
    slots = devices * 4
    group = point_group[:, 0]
    send, idx = build_send(embeddings, group, point_cluster, point_order, slots, dims)
    own = lax.all_to_all(send, ("dp", "blk"), split_axis=0, concat_axis=0, tiled=True)
    forward = [(i, int(nxt[i])) for i in range(devices)]
    backward = [(int(nxt[i]), i) for i in range(devices)]
    query = split_meta(own, width)
    data = query[0]
    labels = jnp.stack([query[1], query[2]])
    prev_data = lax.ppermute(data, ("dp", "blk"), forward)
    next_data = lax.ppermute(data, ("dp", "blk"), backward)
    prev_labels = lax.ppermute(labels, ("dp", "blk"), forward)
    next_labels = lax.ppermute(labels, ("dp", "blk"), backward)
    prev = (prev_data, prev_labels[0], prev_labels[1])
    next_ = (next_data, next_labels[0], next_labels[1])
    best = best_over(query, query)
    near = best_over(query, prev)
    best = jnp.maximum(best, near)
    best = jnp.maximum(best, best_over(query, next_))
    half = slots // 2
    here = lax.axis_index(("dp", "blk"))
    me = jnp.where((here // ys) % 2 == 0, here % ys, (here // (2 * ys)) % xs)
    inner = (me == 1) | (me == 2)
    far_prev = (prev[0],) + lax.optimization_barrier(prev[1:])
    rows = tuple(jnp.where(inner, p[:half], n[half:]) for p, n in zip(far_prev, next_))
    cols = tuple(jnp.where(inner, n, p) for p, n in zip(far_prev, next_))
    scores, same_c, earlier = masks(rows, cols)
    row_part = jnp.max(jnp.where(same_c & earlier, scores, -2.0), axis=1)
    col_ok = same_c & (rows[2][:, None] < cols[2][None, :])
    col_part = jnp.max(jnp.where(col_ok, scores, -2.0), axis=0)
    floor = jnp.full((half,), -2.0, jnp.float32)
    side_prev = jnp.where(inner, jnp.concatenate([row_part, floor]), col_part)
    side_next = jnp.where(inner, col_part, jnp.concatenate([floor, row_part]))
    payload = jnp.concatenate(
        [v.reshape(devices, 1, 4) for v in (best, side_prev, side_next)], axis=2
    )
    returned = lax.all_to_all(
        payload, ("dp", "blk"), split_axis=0, concat_axis=0, tiled=False
    ).reshape(devices * 12)
    at_own, at_prev, at_next = idx[0], idx[1], idx[2]
    entry = jnp.arange(devices * 12, dtype=jnp.int32)[None, :]
    pick = (entry == at_own[:, None]) | (entry == at_prev[:, None]) | (entry == at_next[:, None])
    found = jnp.max(jnp.where(pick, returned[None, :], -2.0), axis=1)
    return jnp.where(found > -1.5, found, -1.0)


def solution(mesh):
    dims = (4, 4, 4)
    nxt, _ = ring_of(*dims)
    in_specs = (P(("dp", "blk"), None), P(("dp", "blk"), None), P(("dp", "blk")), P(("dp", "blk")))
    out_specs = P(("dp", "blk"))

    def run(embeddings, point_group, point_cluster, point_order):
        return body(embeddings, point_group, point_cluster, point_order, nxt, dims)

    return jax.shard_map(run, mesh=mesh, in_specs=in_specs, out_specs=out_specs, check_vma=False)
```

```python
import numpy as np
import jax
import jax.numpy as jnp
from jax import lax
from jax.sharding import PartitionSpec as P
from jax.experimental import pallas as pl

EXTRA = 128


def ring_of(zs, xs, ys):
    def lin(z, x, c, y):
        return ((z * xs + x) * 2 + c) * ys + y

    nxt = np.zeros(zs * xs * 2 * ys, np.int32)
    ring_pos = np.zeros(zs * xs * 2 * ys, np.int32)
    for z in range(zs):
        for x in range(xs):
            for y in range(ys):
                nxt[lin(z, x, 0, y)] = lin(z, x, 0, (y + 1) % ys)
                nxt[lin(z, x, 1, y)] = lin(z, (x + 1) % xs, 1, y)
                ring_pos[lin(z, x, 0, y)] = y
                ring_pos[lin(z, x, 1, y)] = x
    return nxt, ring_pos


def place_of(group, place, zs, xs, ys):
    first = group * 2 * ys + place
    other = group - zs * xs
    second = (((other >> 2) * xs + place) * 2 + 1) * ys + (other & 3)
    return jnp.where(group < zs * xs, first, second)


def prologue(dims):
    zs, xs, ys = dims

    def kernel(emb_ref, group_ref, cluster_ref, order_ref, packed_ref, target_ref, own_ref, prev_ref, next_ref):
        x = emb_ref[...].astype(jnp.float32)
        points, width = x.shape
        scale = lax.rsqrt(jnp.mean(x * x, axis=1, keepdims=True) + 1e-06)
        packed_ref[:, :width] = (x * scale * width ** (-0.5)).astype(jnp.bfloat16)
        group_row = group_ref[...]
        order_row = order_ref[...]
        shape = (packed_ref.shape[1] - width, points)
        which = lax.broadcasted_iota(jnp.int32, shape, 0)
        rows = jnp.where(
            which == 0,
            cluster_ref[...] + 1,
            jnp.where(
                which == 1,
                order_row >> 8,
                jnp.where(which == 2, order_row & 255, jnp.where(which == 3, group_row, 0)),
            ),
        ).astype(jnp.float32)
        cols = rows.T
        packed_ref[:, width:] = cols.astype(jnp.bfloat16)
        group_col = cols[:, 3:4]
        above = lax.broadcasted_iota(jnp.int32, (points, points), 0) < lax.broadcasted_iota(
            jnp.int32, (points, points), 1
        )
        same = (group_col == group_row.astype(jnp.float32)) & above
        rank = jnp.sum(same.astype(jnp.float32), axis=0, keepdims=True).astype(jnp.int32)
        group = group_row
        place = rank >> 2
        lane = rank & 3

        def order_of(lin):
            return (lin & 3) * (2 * zs * xs) + (lin >> 2)

        dev = order_of(place_of(group, place, zs, xs, ys))
        at_prev = order_of(place_of(group, (place + 3) & 3, zs, xs, ys)) * 12 + 8 + lane
        at_next = order_of(place_of(group, (place + 1) & 3, zs, xs, ys)) * 12 + 4 + lane
        target_ref[...] = dev * 4 + lane
        own_ref[...] = dev * 12 + lane
        prev_ref[...] = at_prev
        next_ref[...] = at_next

    return kernel


def build_send(embeddings, group, point_cluster, point_order, slots, dims, interpret=False):
    points, width = embeddings.shape
    packed, target, at_own, at_prev, at_next = pl.pallas_call(
        prologue(dims),
        out_shape=(jax.ShapeDtypeStruct((points, width + EXTRA), jnp.bfloat16),)
        + tuple(jax.ShapeDtypeStruct((1, points), jnp.int32) for _ in range(4)),
        interpret=interpret,
    )(
        embeddings,
        group.reshape(1, points),
        point_cluster.reshape(1, points),
        point_order.reshape(1, points),
    )
    spot = (target.reshape(points)[None, :] == jnp.arange(slots, dtype=jnp.int32)[:, None]).astype(jnp.bfloat16)
    send = lax.dot_general(
        spot, packed, (((1,), (0,)), ((), ())), preferred_element_type=jnp.float32
    ).astype(jnp.bfloat16)
    return send, tuple(a.reshape(points) for a in (at_own, at_prev, at_next))


def split_meta(rows, width):
    cluster = rows[:, width].astype(jnp.float32) - 1.0
    order = rows[:, width + 1].astype(jnp.float32) * 256.0 + rows[:, width + 2].astype(jnp.float32)
    return rows[:, :width], cluster, order


def masks(query, keys):
    query_rows, query_cluster, query_order = query
    key_rows, key_cluster, key_order = keys
    scores = lax.dot_general(
        query_rows, key_rows, (((1,), (1,)), ((), ())), preferred_element_type=jnp.float32
    )
    same = query_cluster[:, None] == key_cluster[None, :]
    return scores, same, key_order[None, :] < query_order[:, None]


def best_over(query, keys):
    scores, same, earlier = masks(query, keys)
    return jnp.max(jnp.where(same & earlier, scores, -2.0), axis=1)


def body(embeddings, point_group, point_cluster, point_order, nxt, dims):
    _, xs, ys = dims
    devices = nxt.shape[0]
    _, width = embeddings.shape
    slots = devices * 4
    group = point_group[:, 0]
    send, idx = build_send(embeddings, group, point_cluster, point_order, slots, dims)
    own = lax.all_to_all(send, ("blk", "dp"), split_axis=0, concat_axis=0, tiled=True)
    forward = [(i, int(nxt[i])) for i in range(devices)]
    backward = [(int(nxt[i]), i) for i in range(devices)]
    query = split_meta(own, width)
    data = query[0]
    labels = jnp.stack([query[1], query[2]])
    prev_data = lax.ppermute(data, ("dp", "blk"), forward)
    next_data = lax.ppermute(data, ("dp", "blk"), backward)
    prev_labels = lax.ppermute(labels, ("dp", "blk"), forward)
    next_labels = lax.ppermute(labels, ("dp", "blk"), backward)
    prev = (prev_data, prev_labels[0], prev_labels[1])
    next_ = (next_data, next_labels[0], next_labels[1])
    best = best_over(query, query)
    best = jnp.maximum(best, best_over(query, prev))
    best = jnp.maximum(best, best_over(query, next_))
    half = slots // 2
    here = lax.axis_index(("dp", "blk"))
    me = jnp.where((here // ys) % 2 == 0, here % ys, (here // (2 * ys)) % xs)
    inner = (me == 1) | (me == 2)
    rows = tuple(jnp.where(inner, p[:half], n[half:]) for p, n in zip(prev, next_))
    cols = tuple(jnp.where(inner, n, p) for p, n in zip(prev, next_))
    scores, same_c, earlier = masks(rows, cols)
    row_part = jnp.max(jnp.where(same_c & earlier, scores, -2.0), axis=1)
    col_ok = same_c & (rows[2][:, None] < cols[2][None, :])
    col_part = jnp.max(jnp.where(col_ok, scores, -2.0), axis=0)
    floor = jnp.full((half,), -2.0, jnp.float32)
    side_prev = jnp.where(inner, jnp.concatenate([row_part, floor]), col_part)
    side_next = jnp.where(inner, col_part, jnp.concatenate([floor, row_part]))
    payload = jnp.concatenate(
        [v.reshape(devices, 1, 4) for v in (best, side_prev, side_next)], axis=2
    )
    returned = lax.all_to_all(
        payload, ("blk", "dp"), split_axis=0, concat_axis=0, tiled=False
    ).reshape(devices * 12)
    at_own, at_prev, at_next = idx[0], idx[1], idx[2]
    entry = jnp.arange(devices * 12, dtype=jnp.int32)[None, :]
    pick = (entry == at_own[:, None]) | (entry == at_prev[:, None]) | (entry == at_next[:, None])
    found = jnp.max(jnp.where(pick, returned[None, :], -2.0), axis=1)
    return jnp.where(found > -1.5, found, -1.0)


def solution(mesh):
    dims = (4, 4, 4)
    nxt, _ = ring_of(*dims)
    in_specs = (P(("dp", "blk"), None), P(("dp", "blk"), None), P(("dp", "blk")), P(("dp", "blk")))
    out_specs = P(("dp", "blk"))

    def run(embeddings, point_group, point_cluster, point_order):
        return body(embeddings, point_group, point_cluster, point_order, nxt, dims)

    return jax.shard_map(run, mesh=mesh, in_specs=in_specs, out_specs=out_specs, check_vma=False)
```

```python
import numpy as np
import jax
import jax.numpy as jnp
from jax import lax
from jax.sharding import PartitionSpec as P
from jax.experimental import pallas as pl

EXTRA = 128


def ring_of(zs, xs, ys):
    def lin(z, x, c, y):
        return ((z * xs + x) * 2 + c) * ys + y

    nxt = np.zeros(zs * xs * 2 * ys, np.int32)
    ring_pos = np.zeros(zs * xs * 2 * ys, np.int32)
    for z in range(zs):
        for x in range(xs):
            for y in range(ys):
                nxt[lin(z, x, 0, y)] = lin(z, x, 0, (y + 1) % ys)
                nxt[lin(z, x, 1, y)] = lin(z, (x + 1) % xs, 1, y)
                ring_pos[lin(z, x, 0, y)] = y
                ring_pos[lin(z, x, 1, y)] = x
    return nxt, ring_pos


def place_of(group, place, zs, xs, ys):
    first = group * 2 * ys + place
    other = group - zs * xs
    second = (((other >> 2) * xs + place) * 2 + 1) * ys + (other & 3)
    return jnp.where(group < zs * xs, first, second)


def prologue(dims):
    zs, xs, ys = dims

    def kernel(emb_ref, group_ref, cluster_ref, order_ref, packed_ref, target_ref, own_ref, prev_ref, next_ref):
        x = emb_ref[...].astype(jnp.float32)
        points, width = x.shape
        scale = lax.rsqrt(jnp.mean(x * x, axis=1, keepdims=True) + 1e-06)
        packed_ref[:, :width] = (x * scale * width ** (-0.5)).astype(jnp.bfloat16)
        group_row = group_ref[...]
        order_row = order_ref[...]
        shape = (packed_ref.shape[1] - width, points)
        which = lax.broadcasted_iota(jnp.int32, shape, 0)
        rows = jnp.where(
            which == 0,
            cluster_ref[...] + 1,
            jnp.where(
                which == 1,
                order_row >> 8,
                jnp.where(which == 2, order_row & 255, jnp.where(which == 3, group_row, 0)),
            ),
        ).astype(jnp.float32)
        cols = rows.T
        packed_ref[:, width:] = cols.astype(jnp.bfloat16)
        group_col = cols[:, 3:4]
        above = lax.broadcasted_iota(jnp.int32, (points, points), 0) < lax.broadcasted_iota(
            jnp.int32, (points, points), 1
        )
        same = (group_col == group_row.astype(jnp.float32)) & above
        rank = jnp.sum(same.astype(jnp.float32), axis=0, keepdims=True).astype(jnp.int32)
        group = group_row
        place = rank >> 2
        lane = rank & 3
        dev = place_of(group, place, zs, xs, ys)
        at_prev = place_of(group, (place + 3) & 3, zs, xs, ys) * 12 + 8 + lane
        at_next = place_of(group, (place + 1) & 3, zs, xs, ys) * 12 + 4 + lane
        target_ref[...] = dev * 4 + lane
        own_ref[...] = dev * 12 + lane
        prev_ref[...] = at_prev
        next_ref[...] = at_next

    return kernel


def build_send(embeddings, group, point_cluster, point_order, slots, dims, interpret=False):
    points, width = embeddings.shape
    packed, target, at_own, at_prev, at_next = pl.pallas_call(
        prologue(dims),
        out_shape=(jax.ShapeDtypeStruct((points, width + EXTRA), jnp.bfloat16),)
        + tuple(jax.ShapeDtypeStruct((1, points), jnp.int32) for _ in range(4)),
        interpret=interpret,
    )(
        embeddings,
        group.reshape(1, points),
        point_cluster.reshape(1, points),
        point_order.reshape(1, points),
    )
    spot = (target.reshape(points)[None, :] == jnp.arange(slots, dtype=jnp.int32)[:, None]).astype(jnp.bfloat16)
    send = lax.dot_general(
        spot, packed, (((1,), (0,)), ((), ())), preferred_element_type=jnp.float32
    ).astype(jnp.bfloat16)
    return send, tuple(a.reshape(points) for a in (at_own, at_prev, at_next))


def split_meta(rows, width):
    cluster = rows[:, width].astype(jnp.float32) - 1.0
    order = rows[:, width + 1].astype(jnp.float32) * 256.0 + rows[:, width + 2].astype(jnp.float32)
    return rows[:, :width], cluster, order


def masks(query, keys):
    query_rows, query_cluster, query_order = query
    key_rows, key_cluster, key_order = keys
    scores = lax.dot_general(
        query_rows, key_rows, (((1,), (1,)), ((), ())), preferred_element_type=jnp.float32
    )
    same = query_cluster[:, None] == key_cluster[None, :]
    return scores, same, key_order[None, :] < query_order[:, None]


def best_over(query, keys):
    scores, same, earlier = masks(query, keys)
    return jnp.max(jnp.where(same & earlier, scores, -2.0), axis=1)


def body(embeddings, point_group, point_cluster, point_order, nxt, dims):
    _, xs, ys = dims
    devices = nxt.shape[0]
    points, width = embeddings.shape
    slots = devices * 4
    group = point_group[:, 0]
    send, idx = build_send(embeddings, group, point_cluster, point_order, slots, dims)
    own = lax.all_to_all(send, ("dp", "blk"), split_axis=0, concat_axis=0, tiled=True)
    forward = [(i, int(nxt[i])) for i in range(devices)]
    backward = [(int(nxt[i]), i) for i in range(devices)]
    query = split_meta(own, width)
    data = query[0]
    labels = jnp.stack([query[1], query[2]])
    prev_data = lax.ppermute(data, ("dp", "blk"), forward)
    next_data = lax.ppermute(data, ("dp", "blk"), backward)
    prev_labels = lax.ppermute(labels, ("dp", "blk"), forward)
    next_labels = lax.ppermute(labels, ("dp", "blk"), backward)
    prev = (prev_data, prev_labels[0], prev_labels[1])
    next_ = (next_data, next_labels[0], next_labels[1])
    best = best_over(query, query)
    best = jnp.maximum(best, best_over(query, prev))
    best = jnp.maximum(best, best_over(query, next_))
    half = slots // 2
    here = lax.axis_index(("dp", "blk"))
    me = jnp.where((here // ys) % 2 == 0, here % ys, (here // (2 * ys)) % xs)
    inner = (me == 1) | (me == 2)
    rows = tuple(jnp.where(inner, p[:half], n[half:]) for p, n in zip(prev, next_))
    cols = tuple(jnp.where(inner, n, p) for p, n in zip(prev, next_))
    scores, same_c, earlier = masks(rows, cols)
    row_part = jnp.max(jnp.where(same_c & earlier, scores, -2.0), axis=1)
    col_ok = same_c & (rows[2][:, None] < cols[2][None, :])
    col_part = jnp.max(jnp.where(col_ok, scores, -2.0), axis=0)
    floor = jnp.full((half,), -2.0, jnp.float32)
    side_prev = jnp.where(inner, jnp.concatenate([row_part, floor]), col_part)
    side_next = jnp.where(inner, col_part, jnp.concatenate([floor, row_part]))
    lanes = 128
    payload = jnp.concatenate(
        [v.reshape(devices, 1, 4) for v in (best, side_prev, side_next)]
        + [jnp.broadcast_to(jnp.minimum(best[0], -2.0), (devices, 1, lanes - 12))],
        axis=2,
    )
    returned = lax.all_to_all(
        payload, ("dp", "blk"), split_axis=0, concat_axis=0, tiled=False
    ).reshape(devices, lanes)
    at = jnp.concatenate(idx)
    sender = (at // 12)[:, None] == jnp.arange(devices, dtype=jnp.int32)[None, :]
    rows = lax.dot_general(
        sender.astype(jnp.float32),
        returned,
        (((1,), (0,)), ((), ())),
        precision=lax.Precision.HIGHEST,
        preferred_element_type=jnp.float32,
    )
    column = (at % 12)[:, None] == jnp.arange(lanes, dtype=jnp.int32)[None, :]
    found = jnp.max(jnp.where(column, rows, -2.0), axis=1).reshape(3, points)
    found = jnp.max(found, axis=0)
    return jnp.where(found > -1.5, found, -1.0)


def solution(mesh):
    dims = (4, 4, 4)
    nxt, _ = ring_of(*dims)
    in_specs = (P(("dp", "blk"), None), P(("dp", "blk"), None), P(("dp", "blk")), P(("dp", "blk")))
    out_specs = P(("dp", "blk"))

    def run(embeddings, point_group, point_cluster, point_order):
        return body(embeddings, point_group, point_cluster, point_order, nxt, dims)

    return jax.shard_map(run, mesh=mesh, in_specs=in_specs, out_specs=out_specs, check_vma=False)
```

```python
import numpy as np
import jax
import jax.numpy as jnp
from jax import lax
from jax.sharding import PartitionSpec as P
from jax.experimental import pallas as pl

EXTRA = 128


def ring_of(zs, xs, ys):
    def lin(z, x, c, y):
        return ((z * xs + x) * 2 + c) * ys + y

    nxt = np.zeros(zs * xs * 2 * ys, np.int32)
    ring_pos = np.zeros(zs * xs * 2 * ys, np.int32)
    for z in range(zs):
        for x in range(xs):
            for y in range(ys):
                nxt[lin(z, x, 0, y)] = lin(z, x, 0, (y + 1) % ys)
                nxt[lin(z, x, 1, y)] = lin(z, (x + 1) % xs, 1, y)
                ring_pos[lin(z, x, 0, y)] = y
                ring_pos[lin(z, x, 1, y)] = x
    return nxt, ring_pos


def place_of(group, place, zs, xs, ys):
    first = group * 2 * ys + place
    other = group - zs * xs
    second = (((other >> 2) * xs + place) * 2 + 1) * ys + (other & 3)
    return jnp.where(group < zs * xs, first, second)


def prologue(dims):
    zs, xs, ys = dims

    def kernel(emb_ref, group_ref, cluster_ref, order_ref, packed_ref, target_ref, own_ref, prev_ref, next_ref):
        x = emb_ref[...].astype(jnp.float32)
        points, width = x.shape
        scale = lax.rsqrt(jnp.mean(x * x, axis=1, keepdims=True) + 1e-06)
        packed_ref[:, :width] = (x * scale * width ** (-0.5)).astype(jnp.bfloat16)
        group_row = group_ref[...]
        order_row = order_ref[...]
        shape = (packed_ref.shape[1] - width, points)
        which = lax.broadcasted_iota(jnp.int32, shape, 0)
        rows = jnp.where(
            which == 0,
            cluster_ref[...] + 1,
            jnp.where(
                which == 1,
                order_row >> 8,
                jnp.where(which == 2, order_row & 255, jnp.where(which == 3, group_row, 0)),
            ),
        ).astype(jnp.float32)
        cols = rows.T
        packed_ref[:, width:] = cols.astype(jnp.bfloat16)
        group_col = cols[:, 3:4]
        above = lax.broadcasted_iota(jnp.int32, (points, points), 0) < lax.broadcasted_iota(
            jnp.int32, (points, points), 1
        )
        same = (group_col == group_row.astype(jnp.float32)) & above
        rank = jnp.sum(same.astype(jnp.float32), axis=0, keepdims=True).astype(jnp.int32)
        group = group_row
        place = rank >> 2
        lane = rank & 3
        dev = place_of(group, place, zs, xs, ys)
        at_prev = place_of(group, (place + 3) & 3, zs, xs, ys) * 12 + 8 + lane
        at_next = place_of(group, (place + 1) & 3, zs, xs, ys) * 12 + 4 + lane
        target_ref[...] = dev * 4 + lane
        own_ref[...] = dev * 12 + lane
        prev_ref[...] = at_prev
        next_ref[...] = at_next

    return kernel


def build_send(embeddings, group, point_cluster, point_order, slots, dims, interpret=False):
    points, width = embeddings.shape
    packed, target, at_own, at_prev, at_next = pl.pallas_call(
        prologue(dims),
        out_shape=(jax.ShapeDtypeStruct((points, width + EXTRA), jnp.bfloat16),)
        + tuple(jax.ShapeDtypeStruct((1, points), jnp.int32) for _ in range(4)),
        interpret=interpret,
    )(
        embeddings,
        group.reshape(1, points),
        point_cluster.reshape(1, points),
        point_order.reshape(1, points),
    )
    spot = (target.reshape(points)[None, :] == jnp.arange(slots, dtype=jnp.int32)[:, None]).astype(jnp.bfloat16)
    send = lax.dot_general(
        spot, packed, (((1,), (0,)), ((), ())), preferred_element_type=jnp.float32
    ).astype(jnp.bfloat16)
    return send, tuple(a.reshape(points) for a in (at_own, at_prev, at_next))


def split_meta(rows, width):
    cluster = rows[:, width].astype(jnp.float32) - 1.0
    order = rows[:, width + 1].astype(jnp.float32) * 256.0 + rows[:, width + 2].astype(jnp.float32)
    return rows[:, :width], cluster, order


def masks(query, keys):
    query_rows, query_cluster, query_order = query
    key_rows, key_cluster, key_order = keys
    scores = lax.dot_general(
        query_rows, key_rows, (((1,), (1,)), ((), ())), preferred_element_type=jnp.float32
    )
    same = query_cluster[:, None] == key_cluster[None, :]
    return scores, same, key_order[None, :] < query_order[:, None]


def best_over(query, keys):
    scores, same, earlier = masks(query, keys)
    return jnp.max(jnp.where(same & earlier, scores, -2.0), axis=1)


def body(embeddings, point_group, point_cluster, point_order, nxt, dims):
    _, xs, ys = dims
    devices = nxt.shape[0]
    points, width = embeddings.shape
    slots = devices * 4
    group = point_group[:, 0]
    send, idx = build_send(embeddings, group, point_cluster, point_order, slots, dims)
    own = lax.all_to_all(send, ("dp", "blk"), split_axis=0, concat_axis=0, tiled=True)
    forward = [(i, int(nxt[i])) for i in range(devices)]
    backward = [(int(nxt[i]), i) for i in range(devices)]
    query = split_meta(own, width)
    data = query[0]
    labels = jnp.stack([query[1], query[2]])
    prev_data = lax.ppermute(data, ("dp", "blk"), forward)
    next_data = lax.ppermute(data, ("dp", "blk"), backward)
    prev_labels = lax.ppermute(labels, ("dp", "blk"), forward)
    next_labels = lax.ppermute(labels, ("dp", "blk"), backward)
    prev = (prev_data, prev_labels[0], prev_labels[1])
    next_ = (next_data, next_labels[0], next_labels[1])
    best = best_over(query, query)
    best = jnp.maximum(best, best_over(query, prev))
    best = jnp.maximum(best, best_over(query, next_))
    half = slots // 2
    here = lax.axis_index(("dp", "blk"))
    me = jnp.where((here // ys) % 2 == 0, here % ys, (here // (2 * ys)) % xs)
    inner = (me == 1) | (me == 2)
    rows = tuple(jnp.where(inner, p[:half], n[half:]) for p, n in zip(prev, next_))
    cols = tuple(jnp.where(inner, n, p) for p, n in zip(prev, next_))
    scores, same_c, earlier = masks(rows, cols)
    row_part = jnp.max(jnp.where(same_c & earlier, scores, -2.0), axis=1)
    col_ok = same_c & (rows[2][:, None] < cols[2][None, :])
    col_part = jnp.max(jnp.where(col_ok, scores, -2.0), axis=0)
    floor = jnp.full((half,), -2.0, jnp.float32)
    side_prev = jnp.where(inner, jnp.concatenate([row_part, floor]), col_part)
    side_next = jnp.where(inner, col_part, jnp.concatenate([floor, row_part]))
    lanes = 128
    payload = jnp.concatenate(
        [v.reshape(devices, 1, 4) for v in (best, side_prev, side_next)]
        + [jnp.broadcast_to(best.reshape(devices, 1, 4)[:, :, :1] * 0.0 - 2.0, (devices, 1, lanes - 12))],
        axis=2,
    )
    returned = lax.all_to_all(
        payload, ("dp", "blk"), split_axis=0, concat_axis=0, tiled=False
    ).reshape(devices, lanes)
    at = jnp.concatenate(idx)
    sender = lax.div(at, 12)[:, None] == jnp.arange(devices, dtype=jnp.int32)[None, :]
    spot = lax.rem(at, 12)
    rows = lax.dot_general(
        sender.astype(jnp.float32),
        returned,
        (((1,), (0,)), ((), ())),
        precision=lax.Precision.HIGHEST,
        preferred_element_type=jnp.float32,
    )
    column = spot[:, None] == jnp.arange(lanes, dtype=jnp.int32)[None, :]
    found = jnp.max(jnp.where(column, rows, -2.0), axis=1).reshape(3, points)
    found = jnp.max(found, axis=0)
    return jnp.where(found > -1.5, found, -1.0)


def solution(mesh):
    dims = (4, 4, 4)
    nxt, _ = ring_of(*dims)
    in_specs = (P(("dp", "blk"), None), P(("dp", "blk"), None), P(("dp", "blk")), P(("dp", "blk")))
    out_specs = P(("dp", "blk"))

    def run(embeddings, point_group, point_cluster, point_order):
        return body(embeddings, point_group, point_cluster, point_order, nxt, dims)

    return jax.shard_map(run, mesh=mesh, in_specs=in_specs, out_specs=out_specs, check_vma=False)
```

```python
import numpy as np
import jax
import jax.numpy as jnp
from jax import lax
from jax.sharding import PartitionSpec as P
from jax.experimental import pallas as pl

EXTRA = 128


def ring_of(zs, xs, ys):
    def lin(z, x, c, y):
        return ((z * xs + x) * 2 + c) * ys + y

    nxt = np.zeros(zs * xs * 2 * ys, np.int32)
    ring_pos = np.zeros(zs * xs * 2 * ys, np.int32)
    for z in range(zs):
        for x in range(xs):
            for y in range(ys):
                nxt[lin(z, x, 0, y)] = lin(z, x, 0, (y + 1) % ys)
                nxt[lin(z, x, 1, y)] = lin(z, (x + 1) % xs, 1, y)
                ring_pos[lin(z, x, 0, y)] = y
                ring_pos[lin(z, x, 1, y)] = x
    return nxt, ring_pos


def place_of(group, place, zs, xs, ys):
    first = group * 2 * ys + place
    other = group - zs * xs
    second = (((other >> 2) * xs + place) * 2 + 1) * ys + (other & 3)
    return jnp.where(group < zs * xs, first, second)


def prologue(dims):
    zs, xs, ys = dims

    def kernel(emb_ref, group_ref, cluster_ref, order_ref, packed_ref, target_ref, own_ref, prev_ref, next_ref):
        x = emb_ref[...].astype(jnp.float32)
        points, width = x.shape
        scale = lax.rsqrt(jnp.mean(x * x, axis=1, keepdims=True) + 1e-06)
        packed_ref[:, :width] = (x * scale * width ** (-0.5)).astype(jnp.bfloat16)
        group_row = group_ref[...]
        order_row = order_ref[...]
        shape = (packed_ref.shape[1] - width, points)
        which = lax.broadcasted_iota(jnp.int32, shape, 0)
        rows = jnp.where(
            which == 0,
            cluster_ref[...] + 1,
            jnp.where(
                which == 1,
                order_row >> 8,
                jnp.where(which == 2, order_row & 255, jnp.where(which == 3, group_row, 0)),
            ),
        ).astype(jnp.float32)
        cols = rows.T
        packed_ref[:, width:] = cols.astype(jnp.bfloat16)
        group_col = cols[:, 3:4]
        above = lax.broadcasted_iota(jnp.int32, (points, points), 0) < lax.broadcasted_iota(
            jnp.int32, (points, points), 1
        )
        same = (group_col == group_row.astype(jnp.float32)) & above
        rank = jnp.sum(same.astype(jnp.float32), axis=0, keepdims=True).astype(jnp.int32)
        group = group_row
        place = rank >> 2
        lane = rank & 3
        dev = place_of(group, place, zs, xs, ys)
        at_prev = place_of(group, (place + 3) & 3, zs, xs, ys) * 12 + 8 + lane
        at_next = place_of(group, (place + 1) & 3, zs, xs, ys) * 12 + 4 + lane
        target_ref[...] = dev * 4 + lane
        own_ref[...] = dev * 12 + lane
        prev_ref[...] = at_prev
        next_ref[...] = at_next

    return kernel


def build_send(embeddings, group, point_cluster, point_order, slots, dims, interpret=False):
    points, width = embeddings.shape
    packed, target, at_own, at_prev, at_next = pl.pallas_call(
        prologue(dims),
        out_shape=(jax.ShapeDtypeStruct((points, width + EXTRA), jnp.bfloat16),)
        + tuple(jax.ShapeDtypeStruct((1, points), jnp.int32) for _ in range(4)),
        interpret=interpret,
    )(
        embeddings,
        group.reshape(1, points),
        point_cluster.reshape(1, points),
        point_order.reshape(1, points),
    )
    spot = (target.reshape(points)[None, :] == jnp.arange(slots, dtype=jnp.int32)[:, None]).astype(jnp.bfloat16)
    send = lax.dot_general(
        spot, packed, (((1,), (0,)), ((), ())), preferred_element_type=jnp.float32
    ).astype(jnp.bfloat16)
    return send, tuple(a.reshape(points) for a in (at_own, at_prev, at_next))


def split_meta(rows, width):
    cluster = rows[:, width].astype(jnp.float32) - 1.0
    order = rows[:, width + 1].astype(jnp.float32) * 256.0 + rows[:, width + 2].astype(jnp.float32)
    return rows[:, :width], cluster, order


def masks(query, keys):
    query_rows, query_cluster, query_order = query
    key_rows, key_cluster, key_order = keys
    scores = lax.dot_general(
        query_rows, key_rows, (((1,), (1,)), ((), ())), preferred_element_type=jnp.float32
    )
    same = query_cluster[:, None] == key_cluster[None, :]
    return scores, same, key_order[None, :] < query_order[:, None]


def best_over(query, keys):
    scores, same, earlier = masks(query, keys)
    return jnp.max(jnp.where(same & earlier, scores, -2.0), axis=1)


def body(embeddings, point_group, point_cluster, point_order, nxt, dims):
    _, xs, ys = dims
    devices = nxt.shape[0]
    points, width = embeddings.shape
    slots = devices * 4
    group = point_group[:, 0]
    send, idx = build_send(embeddings, group, point_cluster, point_order, slots, dims)
    own = lax.all_to_all(send, ("dp", "blk"), split_axis=0, concat_axis=0, tiled=True)
    forward = [(i, int(nxt[i])) for i in range(devices)]
    backward = [(int(nxt[i]), i) for i in range(devices)]
    query = split_meta(own, width)
    data = query[0]
    labels = jnp.stack([query[1], query[2]])
    prev_data = lax.ppermute(data, ("dp", "blk"), forward)
    next_data = lax.ppermute(data, ("dp", "blk"), backward)
    prev_labels = lax.ppermute(labels, ("dp", "blk"), forward)
    next_labels = lax.ppermute(labels, ("dp", "blk"), backward)
    prev = (prev_data, prev_labels[0], prev_labels[1])
    next_ = (next_data, next_labels[0], next_labels[1])
    best = best_over(query, query)
    near = best_over(query, prev)
    best = jnp.maximum(best, near)
    best = jnp.maximum(best, best_over(query, next_))
    half = slots // 2
    here = lax.axis_index(("dp", "blk"))
    me = jnp.where((here // ys) % 2 == 0, here % ys, (here // (2 * ys)) % xs)
    inner = (me == 1) | (me == 2)
    far_prev = (prev[0],) + lax.optimization_barrier(prev[1:])
    rows = tuple(jnp.where(inner, p[:half], n[half:]) for p, n in zip(far_prev, next_))
    cols = tuple(jnp.where(inner, n, p) for p, n in zip(far_prev, next_))
    scores, same_c, earlier = masks(rows, cols)
    row_part = jnp.max(jnp.where(same_c & earlier, scores, -2.0), axis=1)
    col_ok = same_c & (rows[2][:, None] < cols[2][None, :])
    col_part = jnp.max(jnp.where(col_ok, scores, -2.0), axis=0)
    floor = jnp.full((half,), -2.0, jnp.float32)
    side_prev = jnp.where(inner, jnp.concatenate([row_part, floor]), col_part)
    side_next = jnp.where(inner, col_part, jnp.concatenate([floor, row_part]))
    lanes = 128
    payload = jnp.concatenate(
        [v.reshape(devices, 1, 4) for v in (best, side_prev, side_next)]
        + [jnp.broadcast_to(best.reshape(devices, 1, 4)[:, :, :1] * 0.0 - 2.0, (devices, 1, lanes - 12))],
        axis=2,
    )
    returned = lax.all_to_all(
        payload, ("dp", "blk"), split_axis=0, concat_axis=0, tiled=False
    ).reshape(devices, lanes)
    at = jnp.concatenate(idx)
    sender = lax.div(at, 12)[:, None] == jnp.arange(devices, dtype=jnp.int32)[None, :]
    spot = lax.rem(at, 12)
    rows = lax.dot_general(
        sender.astype(jnp.float32),
        returned,
        (((1,), (0,)), ((), ())),
        precision=lax.Precision.HIGHEST,
        preferred_element_type=jnp.float32,
    )
    column = spot[:, None] == jnp.arange(lanes, dtype=jnp.int32)[None, :]
    found = jnp.max(jnp.where(column, rows, -2.0), axis=1).reshape(3, points)
    found = jnp.max(found, axis=0)
    return jnp.where(found > -1.5, found, -1.0)


def solution(mesh):
    dims = (4, 4, 4)
    nxt, _ = ring_of(*dims)
    in_specs = (P(("dp", "blk"), None), P(("dp", "blk"), None), P(("dp", "blk")), P(("dp", "blk")))
    out_specs = P(("dp", "blk"))

    def run(embeddings, point_group, point_cluster, point_order):
        return body(embeddings, point_group, point_cluster, point_order, nxt, dims)

    return jax.shard_map(run, mesh=mesh, in_specs=in_specs, out_specs=out_specs, check_vma=False)
```
